256 devices in a mesh: req: 8 (over x, z_hi), blk: 32 (over y, z_lo, core).
Axes of the slice: x: 4, y: 4, z: 8 (z_hi: 2, z_lo: 4; z = z_hi * 4 + z_lo), core: 2. Of those that a mesh axis runs over, the one named last changes fastest.
Arguments:
- tokens: bfloat16 [256, 128, 1536], P(('req', 'blk')), may hold values from -6 to 6
- cache_kv: bfloat16 [256, 2, 256, 384], P(('req', 'blk')), may hold values from -200 to 200
- cache_len: int32 [256], P(('req', 'blk')), may hold values from 2 to 256, as said below
- holder: int32 [256], P(('req', 'blk')), may hold values from 0 to 7, as said below
- accept: int32 [256, 128], P(('req', 'blk')), may hold values from 0 to 1, as said below
- attn_gain: float32 [1536], replicated, may hold values from 0.1 to 1.9
- q_weight: bfloat16 [1536, 768], replicated, may hold values from -0.15625 to 0.15625
- k_weight: bfloat16 [1536, 384], replicated, may hold values from -0.15625 to 0.15625
- v_weight: bfloat16 [1536, 384], replicated, may hold values from -0.15625 to 0.15625
- o_weight: bfloat16 [768, 1536], replicated, may hold values from -0.21875 to 0.21875
- ffn_gain: float32 [1536], replicated, may hold values from 0.4 to 2.5
- w_gate: bfloat16 [1536, 4096], P(None, 'blk'), may hold values from -0.15625 to 0.15625
- w_up: bfloat16 [1536, 4096], P(None, 'blk'), may hold values from -0.15625 to 0.15625
- w_down: bfloat16 [4096, 1536], P('blk'), may hold values from -0.09375 to 0.09375
Outputs:
- refined: float32 [256, 128, 1536], P(('req', 'blk'))
The draws below stay inside these ranges and needn't reach their ends.
Inputs may be any that keep to these rules, and one draw needn't show every extreme that they name: `holder`: requests whose numbers agree modulo 32 have distinct holders. `cache_len`: some request has exactly 256 cached positions. `accept`: each request accepts exactly 64 positions.
All inputs are finite; a program needn't handle non-finite values.
Results may differ from the reference program's by a relative error of at most 0.04.
Values may be sent and summed in bfloat16 or wider, within the bound.
No kernel may reach another device: no remote copies, remote signals or barrier semaphores. Data moves between devices by JAX's collectives and lax.ppermute only.
A program may use at most 128 MiB of HBM per device.

```python
import math
import jax
import jax.numpy as jnp
from jax import lax

D = 1536
HEADS = 8
KV_HEADS = 4
HEAD = 96
FF = 4096
BLOCK = 128
ACCEPT = 64
CSLOT = 256
QW = 768
KVW = 384
REQ_GROUP = 8
BLK_GROUP = 32
FF_DEV = 128
REQUESTS = 256


def draw_cache_len(key, part):
    first_key, second_key = jax.random.split(key)
    lengths = jax.random.randint(first_key, (REQUESTS,), 2, CSLOT + 1)
    longest = jax.random.randint(second_key, (), 0, REQUESTS)
    return jnp.where(jnp.arange(REQUESTS) == longest, CSLOT, lengths).astype(jnp.int32)


def draw_holder(key, part):
    column_keys = jax.random.split(key, BLK_GROUP)

    def column(column_key):
        return jax.random.permutation(column_key, REQ_GROUP).astype(jnp.int32)
    columns = jax.vmap(column)(column_keys)
    return columns.T.reshape(REQUESTS).astype(jnp.int32)


def draw_accept(key, part):
    row_keys = jax.random.split(key, REQUESTS)

    def one_row(row_key):
        order = jax.random.permutation(row_key, BLOCK)
        return jnp.zeros((BLOCK,), jnp.int32).at[order[:ACCEPT]].set(1)
    return jax.vmap(one_row)(row_keys).astype(jnp.int32)


def draw_cache_kv(key, part):
    base_key = jax.random.fold_in(key, 0)
    shape = (REQUESTS, 2, CSLOT, KVW)
    drawn = jnp.clip(jax.random.normal(base_key, shape, jnp.float32), -6.0, 6.0)
    return drawn.astype(jnp.bfloat16)


def level_of(stream_key, shape, cuts, low, largest):
    def one(dim, parts):
        draws = jax.random.uniform(jax.random.fold_in(jax.random.fold_in(stream_key, 6), dim), (parts,), jnp.float32, low / len(cuts), largest / len(cuts))
        return jnp.repeat(jnp.exp(draws), shape[dim] // parts).reshape((-1,) + (1,) * (len(shape) - dim - 1))

    level = one(*cuts[0])
    for cut in cuts[1:]:
        level = level * one(*cut)
    return level


def bell_draw(key, extent, scale, most, shards=(), held_as=jnp.bfloat16):
    values = scale * jax.random.normal(key, extent, jnp.float32)
    if shards:
        values = values * level_of(key, extent, shards, -0.22, 0.18)
    return jnp.clip(values, -most, most).astype(held_as)


def setup_inputs(seed: int = 0) -> dict:
    key_of = jax.random.split(jax.random.key(seed), 15)
    tokens = bell_draw(key_of[0], (REQUESTS, BLOCK, D), 1.0, 6.0, ((0, 256),))
    cache_kv = draw_cache_kv(jax.random.fold_in(key_of[14], 71), 0)
    cache_len = draw_cache_len(jax.random.fold_in(key_of[14], 71), 0)
    holder = draw_holder(jax.random.fold_in(key_of[14], 71), 0)
    accept = draw_accept(jax.random.fold_in(key_of[14], 71), 0)
    attn_gain = jnp.clip(1.0 + 0.18 * jax.random.normal(key_of[5], (D,), jnp.float32), 0.1, 1.9)
    q_weight = bell_draw(key_of[6], (D, QW), D ** -0.5, 0.15625)
    k_weight = bell_draw(key_of[7], (D, KVW), D ** -0.5, 0.15625)
    v_weight = bell_draw(key_of[8], (D, KVW), D ** -0.5, 0.15625)
    o_weight = bell_draw(key_of[9], (QW, D), QW ** -0.5, 0.21875)
    ffn_gain = jnp.clip(jnp.exp(jax.random.uniform(key_of[10], (D,), jnp.float32, math.log(0.4), math.log(2.5))), 0.4, 2.5)
    w_gate = bell_draw(key_of[11], (D, FF), D ** -0.5, 0.15625, ((1, 32),))
    w_up = bell_draw(key_of[12], (D, FF), D ** -0.5, 0.15625, ((1, 32),))
    w_down = bell_draw(key_of[13], (FF, D), FF ** -0.5, 0.09375, ((0, 32),))
    return dict(tokens=tokens, cache_kv=cache_kv, cache_len=cache_len, holder=holder, accept=accept, attn_gain=attn_gain, q_weight=q_weight, k_weight=k_weight, v_weight=v_weight, o_weight=o_weight, ffn_gain=ffn_gain, w_gate=w_gate, w_up=w_up, w_down=w_down)


norm_eps = 1e-05
rope_base = 100000.0

def rms_scale(values, gain_row):
    return values * lax.rsqrt(lax.optimization_barrier(jnp.mean(values * values, axis=-1, keepdims=True)) + norm_eps) * gain_row

def rotate_heads(flat, positions, head_count):
    half_dim = HEAD // 2
    shaped = flat.reshape(flat.shape[0], head_count, HEAD)
    freqs = jnp.exp(-jnp.log(rope_base) * 2.0 * jnp.arange(half_dim, dtype=jnp.float32) / HEAD)
    angles = positions[:, None] * freqs[None, :]
    cosine = jnp.cos(angles)[:, None, :]
    sine = jnp.sin(angles)[:, None, :]
    first_half = shaped[..., :half_dim]
    second_half = shaped[..., half_dim:]
    turned = jnp.concatenate([first_half * cosine - second_half * sine, second_half * cosine + first_half * sine], axis=-1)
    return turned.reshape(flat.shape[0], head_count * HEAD)

def attend_block(tok_rows, cache_keys, cache_vals, cache_length, attn_gain, q_weight, k_weight, v_weight, o_weight):
    block_len = tok_rows.shape[0]
    slot_len = cache_keys.shape[0]
    widened = tok_rows.astype(jnp.float32)
    normed = rms_scale(widened, attn_gain).astype(jnp.bfloat16)
    positions = (cache_length + jnp.arange(block_len, dtype=jnp.int32)).astype(jnp.float32)
    queries = rotate_heads(jnp.dot(normed, q_weight, preferred_element_type=jnp.float32), positions, HEADS).astype(jnp.bfloat16)
    new_keys = rotate_heads(jnp.dot(normed, k_weight, preferred_element_type=jnp.float32), positions, KV_HEADS).astype(jnp.bfloat16)
    new_vals = jnp.dot(normed, v_weight, preferred_element_type=jnp.float32).astype(jnp.bfloat16)
    all_keys = jnp.concatenate([cache_keys, new_keys], axis=0).reshape(slot_len + block_len, KV_HEADS, HEAD)
    all_vals = jnp.concatenate([cache_vals, new_vals], axis=0).reshape(slot_len + block_len, KV_HEADS, HEAD)
    grouped = queries.reshape(block_len, KV_HEADS, HEADS // KV_HEADS, HEAD)
    scores = jnp.einsum('bgid,kgd->gibk', grouped.astype(jnp.float32), all_keys.astype(jnp.float32)) * HEAD ** (-0.5)
    valid = jnp.concatenate([jnp.arange(slot_len, dtype=jnp.int32) < cache_length, jnp.ones((block_len,), dtype=jnp.bool_)])
    scores = jnp.where(valid, scores, -jnp.inf)
    peaks = lax.optimization_barrier(jnp.max(scores, axis=-1, keepdims=True))
    expd = jnp.exp(scores - peaks)
    probs = (expd / lax.optimization_barrier(jnp.sum(expd, axis=-1, keepdims=True))).astype(jnp.bfloat16)
    context = jnp.einsum('gibk,kgd->bgid', probs.astype(jnp.float32), all_vals.astype(jnp.float32))
    context = context.astype(jnp.bfloat16).reshape(block_len, HEADS * HEAD)
    return widened + jnp.dot(context, o_weight, preferred_element_type=jnp.float32)

def reference(tokens, cache_kv, cache_len, holder, accept, attn_gain, q_weight, k_weight, v_weight, o_weight, ffn_gain, w_gate, w_up, w_down):
    source = holder * BLK_GROUP + jnp.arange(REQUESTS, dtype=jnp.int32) % BLK_GROUP
    fetched = cache_kv[source]
    cache_keys = fetched[:, 0]
    cache_vals = fetched[:, 1]

    def one_pass(states):
        return jax.vmap(attend_block, in_axes=(0, 0, 0, 0, None, None, None, None, None))(states, cache_keys, cache_vals, cache_len, attn_gain, q_weight, k_weight, v_weight, o_weight)
    first = one_pass(tokens)
    flat_first = first.reshape(REQUESTS * BLOCK, D)
    fnorm = rms_scale(flat_first, ffn_gain).astype(jnp.bfloat16)

    def add_group(total, group_index):
        offset = group_index * FF_DEV
        gate_cols = lax.dynamic_slice_in_dim(w_gate, offset, FF_DEV, 1)
        up_cols = lax.dynamic_slice_in_dim(w_up, offset, FF_DEV, 1)
        down_rows = lax.dynamic_slice_in_dim(w_down, offset, FF_DEV, 0)
        gate_vals = jnp.dot(fnorm, gate_cols, preferred_element_type=jnp.float32)
        up_vals = jnp.dot(fnorm, up_cols, preferred_element_type=jnp.float32)
        hidden = (jax.nn.silu(gate_vals) * up_vals).astype(jnp.bfloat16)
        partial_term = jnp.dot(hidden, down_rows, preferred_element_type=jnp.float32).astype(jnp.bfloat16)
        partial_term = lax.optimization_barrier(partial_term)
        return (total + partial_term.astype(jnp.float32), None)
    ffn_out, _ = lax.scan(add_group, jnp.zeros((REQUESTS * BLOCK, D), jnp.float32), jnp.arange(BLK_GROUP, dtype=jnp.int32))
    draft = (flat_first + ffn_out).reshape(REQUESTS, BLOCK, D)
    second_in = jnp.where((accept == 1)[:, :, None], draft, tokens.astype(jnp.float32))
    return one_pass(second_in)
```

```python
import jax
import jax.numpy as jnp
from jax import lax
from jax.sharding import PartitionSpec as P

HEAD = 96


norm_eps = 1e-05
rope_base = 100000.0


def rms_scale(values, gain_row):
    return (
        values * lax.rsqrt(jnp.mean(values * values, axis=-1, keepdims=True) + norm_eps) * gain_row
    )


def rotate_heads(flat, positions, head_count):
    half_dim = HEAD // 2
    shaped = flat.reshape(flat.shape[0], head_count, HEAD)
    freqs = jnp.exp(-jnp.log(rope_base) * 2.0 * jnp.arange(half_dim, dtype=jnp.float32) / HEAD)
    angles = positions[:, None] * freqs[None, :]
    cosine = jnp.cos(angles)[:, None, :]
    sine = jnp.sin(angles)[:, None, :]
    first_half = shaped[..., :half_dim]
    second_half = shaped[..., half_dim:]
    turned = jnp.concatenate(
        [first_half * cosine - second_half * sine, second_half * cosine + first_half * sine],
        axis=-1,
    )
    return turned.reshape(flat.shape[0], head_count * HEAD)


def attend_block(
    tok_rows,
    cache_keys,
    cache_vals,
    cache_length,
    attn_gain,
    q_weight,
    k_weight,
    v_weight,
    o_weight,
):
    block_len = tok_rows.shape[0]
    slot_len = cache_keys.shape[0]
    kv_count = k_weight.shape[1] // HEAD
    q_count = q_weight.shape[1] // HEAD
    widened = tok_rows.astype(jnp.float32)
    normed = rms_scale(widened, attn_gain).astype(jnp.bfloat16)
    positions = (cache_length + jnp.arange(block_len, dtype=jnp.int32)).astype(jnp.float32)
    queries = rotate_heads(
        jnp.dot(normed, q_weight, preferred_element_type=jnp.float32), positions, q_count
    ).astype(jnp.bfloat16)
    new_keys = rotate_heads(
        jnp.dot(normed, k_weight, preferred_element_type=jnp.float32), positions, kv_count
    ).astype(jnp.bfloat16)
    new_vals = jnp.dot(normed, v_weight, preferred_element_type=jnp.float32).astype(jnp.bfloat16)
    all_keys = jnp.concatenate([cache_keys, new_keys], axis=0).reshape(
        slot_len + block_len, kv_count, HEAD
    )
    all_vals = jnp.concatenate([cache_vals, new_vals], axis=0).reshape(
        slot_len + block_len, kv_count, HEAD
    )
    grouped = queries.reshape(block_len, kv_count, q_count // kv_count, HEAD)
    scores = jnp.einsum(
        "bgid,kgd->gibk", grouped, all_keys, preferred_element_type=jnp.float32
    ) * HEAD ** (-0.5)
    valid = jnp.concatenate(
        [
            jnp.arange(slot_len, dtype=jnp.int32) < cache_length,
            jnp.ones((block_len,), dtype=jnp.bool_),
        ]
    )
    scores = jnp.where(valid, scores, -jnp.inf)
    peaks = jnp.max(scores, axis=-1, keepdims=True)
    expd = jnp.exp(scores - peaks)
    probs = (expd / jnp.sum(expd, axis=-1, keepdims=True)).astype(jnp.bfloat16)
    context = jnp.einsum("gibk,kgd->bgid", probs, all_vals, preferred_element_type=jnp.float32)
    context = context.astype(jnp.bfloat16).reshape(block_len, q_count * HEAD)
    return widened + jnp.dot(context, o_weight, preferred_element_type=jnp.float32)


def run_ffn(normed_rows, w_gate, w_up, w_down, down_all):
    part_rows = lax.all_gather(normed_rows, "blk", axis=0, tiled=True)
    gate_vals = jnp.dot(part_rows, w_gate, preferred_element_type=jnp.float32)
    up_vals = jnp.dot(part_rows, w_up, preferred_element_type=jnp.float32)
    hidden_all = (jax.nn.silu(gate_vals) * up_vals).astype(jnp.bfloat16)
    hidden_own = lax.all_to_all(hidden_all, "blk", 0, 1, tiled=True)
    groups = w_down.shape[0]
    group_count = down_all.shape[0] // groups
    terms = jnp.einsum(
        "rgk,gkd->grd",
        hidden_own.reshape(hidden_own.shape[0], group_count, groups),
        down_all.reshape(group_count, groups, down_all.shape[1]),
        preferred_element_type=jnp.float32,
    ).astype(jnp.bfloat16)
    return jnp.sum(terms.astype(jnp.float32), axis=0)


def fetch_slot(cache_kv, holder):
    count = lax.axis_size("req")
    own = cache_kv[0]
    holders = lax.all_gather(holder, "req", axis=0, tiled=True)
    if count != 8:
        slots = lax.all_gather(own, "req", axis=0, tiled=False)
        return slots[holder[0]]
    me = lax.axis_index("req")

    def swap(values, mask):
        return lax.ppermute(values, "req", perm=[(i, i ^ mask) for i in range(count)])

    def pick(cond, a, b):
        return jnp.where(cond, a, b)

    got1 = swap(own, 4)
    target = me ^ 2
    send_a = pick(holders[target] == (me ^ 4), got1, own)
    send_b = pick(holders[target ^ 1] == (me ^ 4), got1, own)
    got2 = swap(jnp.stack([send_a, send_b]), 2)
    want = holders[me ^ 1]
    send_c = pick(want == me, own, pick(want == (me ^ 4), got1, got2[1]))
    got3 = swap(send_c, 1)
    need = holders[me]
    return pick(
        need == me,
        own,
        pick(need == (me ^ 4), got1, pick((need ^ me) == 2, got2[0], pick((need ^ me) == 6, got2[0], got3))),
    )


def local(
    tokens,
    cache_kv,
    cache_len,
    holder,
    accept,
    attn_gain,
    q_weight,
    k_weight,
    v_weight,
    o_weight,
    ffn_gain,
    w_gate,
    w_up,
    w_down,
):
    fetched = fetch_slot(cache_kv, holder)
    down_all = lax.all_gather(w_down, "blk", axis=0, tiled=True)
    fetched, down_all = lax.optimization_barrier((fetched, down_all))
    cache_keys = fetched[0]
    cache_vals = fetched[1]
    cache_length = cache_len[0]
    block_rows = tokens[0]
    first_pass = attend_block(
        block_rows,
        cache_keys,
        cache_vals,
        cache_length,
        attn_gain,
        q_weight,
        k_weight,
        v_weight,
        o_weight,
    )
    chosen_mask = accept[0] == 1
    ffn_sum = run_ffn(rms_scale(first_pass, ffn_gain).astype(jnp.bfloat16), w_gate, w_up, w_down, down_all)
    placed = first_pass + ffn_sum
    second_in = jnp.where(chosen_mask[:, None], placed, block_rows.astype(jnp.float32))
    refined = attend_block(
        second_in,
        cache_keys,
        cache_vals,
        cache_length,
        attn_gain,
        q_weight,
        k_weight,
        v_weight,
        o_weight,
    )
    return refined[None]


def solution(mesh):
    return jax.shard_map(
        local,
        mesh=mesh,
        in_specs=(
            P(("req", "blk"), None, None),
            P(("req", "blk"), None, None, None),
            P(("req", "blk")),
            P(("req", "blk")),
            P(("req", "blk"), None),
            P(),
            P(),
            P(),
            P(),
            P(),
            P(),
            P(None, "blk"),
            P(None, "blk"),
            P("blk", None),
        ),
        out_specs=P(("req", "blk"), None, None),
        check_vma=False,
    )
```

```python
import jax
import jax.numpy as jnp
from jax import lax
from jax.sharding import PartitionSpec as P

HEAD = 96


norm_eps = 1e-05
rope_base = 100000.0


def rms_scale(values, gain_row):
    return (
        values * lax.rsqrt(jnp.mean(values * values, axis=-1, keepdims=True) + norm_eps) * gain_row
    )


def rotate_heads(flat, positions, head_count):
    half_dim = HEAD // 2
    shaped = flat.reshape(flat.shape[0], head_count, HEAD)
    freqs = jnp.exp(-jnp.log(rope_base) * 2.0 * jnp.arange(half_dim, dtype=jnp.float32) / HEAD)
    angles = positions[:, None] * freqs[None, :]
    cosine = jnp.cos(angles)[:, None, :]
    sine = jnp.sin(angles)[:, None, :]
    first_half = shaped[..., :half_dim]
    second_half = shaped[..., half_dim:]
    turned = jnp.concatenate(
        [first_half * cosine - second_half * sine, second_half * cosine + first_half * sine],
        axis=-1,
    )
    return turned.reshape(flat.shape[0], head_count * HEAD)


def attend_block(
    tok_rows,
    cache_keys,
    cache_vals,
    cache_length,
    attn_gain,
    q_weight,
    k_weight,
    v_weight,
    o_weight,
):
    block_len = tok_rows.shape[0]
    slot_len = cache_keys.shape[0]
    kv_count = k_weight.shape[1] // HEAD
    q_count = q_weight.shape[1] // HEAD
    widened = tok_rows.astype(jnp.float32)
    normed = rms_scale(widened, attn_gain).astype(jnp.bfloat16)
    positions = (cache_length + jnp.arange(block_len, dtype=jnp.int32)).astype(jnp.float32)
    queries = rotate_heads(
        jnp.dot(normed, q_weight, preferred_element_type=jnp.float32), positions, q_count
    ).astype(jnp.bfloat16)
    new_keys = rotate_heads(
        jnp.dot(normed, k_weight, preferred_element_type=jnp.float32), positions, kv_count
    ).astype(jnp.bfloat16)
    new_vals = jnp.dot(normed, v_weight, preferred_element_type=jnp.float32).astype(jnp.bfloat16)
    all_keys = jnp.concatenate([cache_keys, new_keys], axis=0).reshape(
        slot_len + block_len, kv_count, HEAD
    )
    all_vals = jnp.concatenate([cache_vals, new_vals], axis=0).reshape(
        slot_len + block_len, kv_count, HEAD
    )
    grouped = queries.reshape(block_len, kv_count, q_count // kv_count, HEAD)
    scores = jnp.einsum(
        "bgid,kgd->gibk", grouped, all_keys, preferred_element_type=jnp.float32
    ) * HEAD ** (-0.5)
    valid = jnp.concatenate(
        [
            jnp.arange(slot_len, dtype=jnp.int32) < cache_length,
            jnp.ones((block_len,), dtype=jnp.bool_),
        ]
    )
    scores = jnp.where(valid, scores, -jnp.inf)
    peaks = jnp.max(scores, axis=-1, keepdims=True)
    expd = jnp.exp(scores - peaks)
    probs = (expd / jnp.sum(expd, axis=-1, keepdims=True)).astype(jnp.bfloat16)
    context = jnp.einsum("gibk,kgd->bgid", probs, all_vals, preferred_element_type=jnp.float32)
    context = context.astype(jnp.bfloat16).reshape(block_len, q_count * HEAD)
    return widened + jnp.dot(context, o_weight, preferred_element_type=jnp.float32)


def run_ffn(normed_rows, w_gate, w_up, w_down, down_all):
    part_rows = lax.all_gather(normed_rows, "blk", axis=0, tiled=True)
    gate_vals = jnp.dot(part_rows, w_gate, preferred_element_type=jnp.float32)
    up_vals = jnp.dot(part_rows, w_up, preferred_element_type=jnp.float32)
    hidden_all = (jax.nn.silu(gate_vals) * up_vals).astype(jnp.bfloat16)
    hidden_own = lax.all_to_all(hidden_all, "blk", 0, 1, tiled=True)
    groups = w_down.shape[0]
    group_count = down_all.shape[0] // groups
    terms = jnp.einsum(
        "rgk,gkd->grd",
        hidden_own.reshape(hidden_own.shape[0], group_count, groups),
        down_all.reshape(group_count, groups, down_all.shape[1]),
        preferred_element_type=jnp.float32,
    ).astype(jnp.bfloat16)
    return jnp.sum(terms.astype(jnp.float32), axis=0)


def fetch_slot(cache_kv, holder):
    count = lax.axis_size("req")
    own = cache_kv[0]
    if count != 8:
        slots = lax.all_gather(own, "req", axis=0, tiled=False)
        return slots[holder[0]]
    me = lax.axis_index("req")

    def swap(values, mask):
        return lax.ppermute(values, "req", perm=[(i, i ^ mask) for i in range(count)])

    def pick(cond, a, b):
        return jnp.where(cond, a, b)

    near = swap(holder, 1)
    quad = swap(jnp.concatenate([holder, near]), 2)
    holders = {0: holder[0], 1: near[0], 2: quad[0], 3: quad[1]}

    got1 = swap(own, 4)
    send_a = pick(holders[2] == (me ^ 4), got1, own)
    send_b = pick(holders[3] == (me ^ 4), got1, own)
    got2 = swap(jnp.stack([send_a, send_b]), 2)
    want = holders[1]
    send_c = pick(want == me, own, pick(want == (me ^ 4), got1, got2[1]))
    got3 = swap(send_c, 1)
    need = holders[0]
    return pick(
        need == me,
        own,
        pick(need == (me ^ 4), got1, pick((need ^ me) == 2, got2[0], pick((need ^ me) == 6, got2[0], got3))),
    )


def local(
    tokens,
    cache_kv,
    cache_len,
    holder,
    accept,
    attn_gain,
    q_weight,
    k_weight,
    v_weight,
    o_weight,
    ffn_gain,
    w_gate,
    w_up,
    w_down,
):
    fetched = fetch_slot(cache_kv, holder)
    copies = jnp.broadcast_to(w_down[None], (lax.axis_size("blk"),) + w_down.shape)
    down_all = lax.all_to_all(copies, "blk", 0, 0, tiled=True).reshape(-1, w_down.shape[1])
    fetched, down_all = lax.optimization_barrier((fetched, down_all))
    cache_keys = fetched[0]
    cache_vals = fetched[1]
    cache_length = cache_len[0]
    block_rows = tokens[0]
    first_pass = attend_block(
        block_rows,
        cache_keys,
        cache_vals,
        cache_length,
        attn_gain,
        q_weight,
        k_weight,
        v_weight,
        o_weight,
    )
    chosen_mask = accept[0] == 1
    ffn_sum = run_ffn(rms_scale(first_pass, ffn_gain).astype(jnp.bfloat16), w_gate, w_up, w_down, down_all)
    placed = first_pass + ffn_sum
    second_in = jnp.where(chosen_mask[:, None], placed, block_rows.astype(jnp.float32))
    refined = attend_block(
        second_in,
        cache_keys,
        cache_vals,
        cache_length,
        attn_gain,
        q_weight,
        k_weight,
        v_weight,
        o_weight,
    )
    return refined[None]


def solution(mesh):
    return jax.shard_map(
        local,
        mesh=mesh,
        in_specs=(
            P(("req", "blk"), None, None),
            P(("req", "blk"), None, None, None),
            P(("req", "blk")),
            P(("req", "blk")),
            P(("req", "blk"), None),
            P(),
            P(),
            P(),
            P(),
            P(),
            P(),
            P(None, "blk"),
            P(None, "blk"),
            P("blk", None),
        ),
        out_specs=P(("req", "blk"), None, None),
        check_vma=False,
    )
```

```python
import jax
import jax.numpy as jnp
from jax import lax
from jax.sharding import PartitionSpec as P

HEAD = 96


norm_eps = 1e-05
rope_base = 100000.0


def rms_scale(values, gain_row):
    return (
        values * lax.rsqrt(jnp.mean(values * values, axis=-1, keepdims=True) + norm_eps) * gain_row
    )


def rotate_heads(flat, positions, head_count):
    half_dim = HEAD // 2
    shaped = flat.reshape(flat.shape[0], head_count, HEAD)
    freqs = jnp.exp(-jnp.log(rope_base) * 2.0 * jnp.arange(half_dim, dtype=jnp.float32) / HEAD)
    angles = positions[:, None] * freqs[None, :]
    cosine = jnp.cos(angles)[:, None, :]
    sine = jnp.sin(angles)[:, None, :]
    first_half = shaped[..., :half_dim]
    second_half = shaped[..., half_dim:]
    turned = jnp.concatenate(
        [first_half * cosine - second_half * sine, second_half * cosine + first_half * sine],
        axis=-1,
    )
    return turned.reshape(flat.shape[0], head_count * HEAD)


def attend_block(
    tok_rows,
    cache_keys,
    cache_vals,
    cache_length,
    attn_gain,
    q_weight,
    k_weight,
    v_weight,
    o_weight,
):
    block_len = tok_rows.shape[0]
    slot_len = cache_keys.shape[0]
    kv_count = k_weight.shape[1] // HEAD
    q_count = q_weight.shape[1] // HEAD
    widened = tok_rows.astype(jnp.float32)
    normed = rms_scale(widened, attn_gain).astype(jnp.bfloat16)
    positions = (cache_length + jnp.arange(block_len, dtype=jnp.int32)).astype(jnp.float32)
    queries = rotate_heads(
        jnp.dot(normed, q_weight, preferred_element_type=jnp.float32), positions, q_count
    ).astype(jnp.bfloat16)
    new_keys = rotate_heads(
        jnp.dot(normed, k_weight, preferred_element_type=jnp.float32), positions, kv_count
    ).astype(jnp.bfloat16)
    new_vals = jnp.dot(normed, v_weight, preferred_element_type=jnp.float32).astype(jnp.bfloat16)
    all_keys = jnp.concatenate([cache_keys, new_keys], axis=0).reshape(
        slot_len + block_len, kv_count, HEAD
    )
    all_vals = jnp.concatenate([cache_vals, new_vals], axis=0).reshape(
        slot_len + block_len, kv_count, HEAD
    )
    grouped = queries.reshape(block_len, kv_count, q_count // kv_count, HEAD)
    scores = jnp.einsum(
        "bgid,kgd->gibk", grouped, all_keys, preferred_element_type=jnp.float32
    ) * HEAD ** (-0.5)
    valid = jnp.concatenate(
        [
            jnp.arange(slot_len, dtype=jnp.int32) < cache_length,
            jnp.ones((block_len,), dtype=jnp.bool_),
        ]
    )
    scores = jnp.where(valid, scores, -jnp.inf)
    peaks = jnp.max(scores, axis=-1, keepdims=True)
    expd = jnp.exp(scores - peaks)
    probs = (expd / jnp.sum(expd, axis=-1, keepdims=True)).astype(jnp.bfloat16)
    context = jnp.einsum("gibk,kgd->bgid", probs, all_vals, preferred_element_type=jnp.float32)
    context = context.astype(jnp.bfloat16).reshape(block_len, q_count * HEAD)
    return widened + jnp.dot(context, o_weight, preferred_element_type=jnp.float32)


def run_ffn(normed_rows, w_gate, w_up, w_down, down_head):
    part_rows = lax.all_gather(normed_rows, "blk", axis=0, tiled=True)
    split = down_head.shape[1]
    tail_cols, part_rows = lax.optimization_barrier((w_down[:, split:], part_rows))
    down_tail = lax.all_gather(tail_cols, "blk", axis=0, tiled=True)
    gate_vals = jnp.dot(part_rows, w_gate, preferred_element_type=jnp.float32)
    up_vals = jnp.dot(part_rows, w_up, preferred_element_type=jnp.float32)
    hidden_all = (jax.nn.silu(gate_vals) * up_vals).astype(jnp.bfloat16)
    hidden_own = lax.all_to_all(hidden_all, "blk", 0, 1, tiled=True)
    groups = w_down.shape[0]
    group_count = down_head.shape[0] // groups
    shaped = hidden_own.reshape(hidden_own.shape[0], group_count, groups)

    def down(cols):
        terms = jnp.einsum(
            "rgk,gkd->grd",
            shaped,
            cols.reshape(group_count, groups, cols.shape[1]),
            preferred_element_type=jnp.float32,
        ).astype(jnp.bfloat16)
        return jnp.sum(terms.astype(jnp.float32), axis=0)

    return jnp.concatenate([down(down_head), down(down_tail)], axis=1)


def fetch_slot(cache_kv, holder):
    count = lax.axis_size("req")
    own = cache_kv[0]
    if count != 8:
        slots = lax.all_gather(own, "req", axis=0, tiled=False)
        return slots[holder[0]]
    me = lax.axis_index("req")

    def swap(values, mask):
        return lax.ppermute(values, "req", perm=[(i, i ^ mask) for i in range(count)])

    def pick(cond, a, b):
        return jnp.where(cond, a, b)

    near = swap(holder, 1)
    quad = swap(jnp.concatenate([holder, near]), 2)
    holders = {0: holder[0], 1: near[0], 2: quad[0], 3: quad[1]}

    got1 = swap(own, 4)
    send_a = pick(holders[2] == (me ^ 4), got1, own)
    send_b = pick(holders[3] == (me ^ 4), got1, own)
    got2 = swap(jnp.stack([send_a, send_b]), 2)
    want = holders[1]
    send_c = pick(want == me, own, pick(want == (me ^ 4), got1, got2[1]))
    got3 = swap(send_c, 1)
    need = holders[0]
    return pick(
        need == me,
        own,
        pick(need == (me ^ 4), got1, pick((need ^ me) == 2, got2[0], pick((need ^ me) == 6, got2[0], got3))),
    )


def local(
    tokens,
    cache_kv,
    cache_len,
    holder,
    accept,
    attn_gain,
    q_weight,
    k_weight,
    v_weight,
    o_weight,
    ffn_gain,
    w_gate,
    w_up,
    w_down,
):
    fetched = fetch_slot(cache_kv, holder)
    split = min(w_down.shape[1], 128 * ((w_down.shape[1] * 7 // 12 + 127) // 128))
    down_head = lax.all_gather(w_down[:, :split], "blk", axis=0, tiled=True)
    fetched, down_head = lax.optimization_barrier((fetched, down_head))
    cache_keys = fetched[0]
    cache_vals = fetched[1]
    cache_length = cache_len[0]
    block_rows = tokens[0]
    first_pass = attend_block(
        block_rows,
        cache_keys,
        cache_vals,
        cache_length,
        attn_gain,
        q_weight,
        k_weight,
        v_weight,
        o_weight,
    )
    chosen_mask = accept[0] == 1
    ffn_sum = run_ffn(rms_scale(first_pass, ffn_gain).astype(jnp.bfloat16), w_gate, w_up, w_down, down_head)
    placed = first_pass + ffn_sum
    second_in = jnp.where(chosen_mask[:, None], placed, block_rows.astype(jnp.float32))
    refined = attend_block(
        second_in,
        cache_keys,
        cache_vals,
        cache_length,
        attn_gain,
        q_weight,
        k_weight,
        v_weight,
        o_weight,
    )
    return refined[None]


def solution(mesh):
    return jax.shard_map(
        local,
        mesh=mesh,
        in_specs=(
            P(("req", "blk"), None, None),
            P(("req", "blk"), None, None, None),
            P(("req", "blk")),
            P(("req", "blk")),
            P(("req", "blk"), None),
            P(),
            P(),
            P(),
            P(),
            P(),
            P(),
            P(None, "blk"),
            P(None, "blk"),
            P("blk", None),
        ),
        out_specs=P(("req", "blk"), None, None),
        check_vma=False,
    )
```

```python
import jax
import jax.numpy as jnp
from jax import lax
from jax.sharding import PartitionSpec as P

HEAD = 96


norm_eps = 1e-05
rope_base = 100000.0


def rms_scale(values, gain_row):
    return (
        values * lax.rsqrt(jnp.mean(values * values, axis=-1, keepdims=True) + norm_eps) * gain_row
    )


def rotate_heads(flat, positions, head_count):
    half_dim = HEAD // 2
    shaped = flat.reshape(flat.shape[0], head_count, HEAD)
    freqs = jnp.exp(-jnp.log(rope_base) * 2.0 * jnp.arange(half_dim, dtype=jnp.float32) / HEAD)
    angles = positions[:, None] * freqs[None, :]
    cosine = jnp.cos(angles)[:, None, :]
    sine = jnp.sin(angles)[:, None, :]
    first_half = shaped[..., :half_dim]
    second_half = shaped[..., half_dim:]
    turned = jnp.concatenate(
        [first_half * cosine - second_half * sine, second_half * cosine + first_half * sine],
        axis=-1,
    )
    return turned.reshape(flat.shape[0], head_count * HEAD)


def attend_block(
    tok_rows,
    cache_keys,
    cache_vals,
    cache_length,
    attn_gain,
    q_weight,
    k_weight,
    v_weight,
    o_weight,
):
    block_len = tok_rows.shape[0]
    slot_len = cache_keys.shape[0]
    kv_count = k_weight.shape[1] // HEAD
    q_count = q_weight.shape[1] // HEAD
    widened = tok_rows.astype(jnp.float32)
    normed = rms_scale(widened, attn_gain).astype(jnp.bfloat16)
    positions = (cache_length + jnp.arange(block_len, dtype=jnp.int32)).astype(jnp.float32)
    queries = rotate_heads(
        jnp.dot(normed, q_weight, preferred_element_type=jnp.float32), positions, q_count
    ).astype(jnp.bfloat16)
    new_keys = rotate_heads(
        jnp.dot(normed, k_weight, preferred_element_type=jnp.float32), positions, kv_count
    ).astype(jnp.bfloat16)
    new_vals = jnp.dot(normed, v_weight, preferred_element_type=jnp.float32).astype(jnp.bfloat16)
    all_keys = jnp.concatenate([cache_keys, new_keys], axis=0).reshape(
        slot_len + block_len, kv_count, HEAD
    )
    all_vals = jnp.concatenate([cache_vals, new_vals], axis=0).reshape(
        slot_len + block_len, kv_count, HEAD
    )
    grouped = queries.reshape(block_len, kv_count, q_count // kv_count, HEAD)
    scores = jnp.einsum(
        "bgid,kgd->gibk", grouped, all_keys, preferred_element_type=jnp.float32
    ) * HEAD ** (-0.5)
    valid = jnp.concatenate(
        [
            jnp.arange(slot_len, dtype=jnp.int32) < cache_length,
            jnp.ones((block_len,), dtype=jnp.bool_),
        ]
    )
    scores = jnp.where(valid, scores, -jnp.inf)
    peaks = jnp.max(scores, axis=-1, keepdims=True)
    expd = jnp.exp(scores - peaks)
    probs = (expd / jnp.sum(expd, axis=-1, keepdims=True)).astype(jnp.bfloat16)
    context = jnp.einsum("gibk,kgd->bgid", probs, all_vals, preferred_element_type=jnp.float32)
    context = context.astype(jnp.bfloat16).reshape(block_len, q_count * HEAD)
    return widened + jnp.dot(context, o_weight, preferred_element_type=jnp.float32)


def gather_ffn_weights(w_gate, w_up, w_down):
    width = w_down.shape[1]
    packed = jnp.concatenate([w_gate.T, w_up.T, w_down], axis=1)
    full = lax.all_gather(packed, "blk", axis=0, tiled=True)
    return full[:, :width], full[:, width : 2 * width], full[:, 2 * width :]


def run_ffn(normed_rows, gate_t, up_t, down_all, groups):
    contract = (((1,), (1,)), ((), ()))
    gate_vals = lax.dot_general(normed_rows, gate_t, contract, preferred_element_type=jnp.float32)
    up_vals = lax.dot_general(normed_rows, up_t, contract, preferred_element_type=jnp.float32)
    hidden = (jax.nn.silu(gate_vals) * up_vals).astype(jnp.bfloat16)
    group_count = down_all.shape[0] // groups
    terms = jnp.einsum(
        "rgk,gkd->grd",
        hidden.reshape(hidden.shape[0], group_count, groups),
        down_all.reshape(group_count, groups, down_all.shape[1]),
        preferred_element_type=jnp.float32,
    ).astype(jnp.bfloat16)
    return jnp.sum(terms.astype(jnp.float32), axis=0)


def fetch_slot(cache_kv, holder):
    count = lax.axis_size("req")
    own = cache_kv[0]
    if count != 8:
        slots = lax.all_gather(own, "req", axis=0, tiled=False)
        return slots[holder[0]]
    me = lax.axis_index("req")

    def swap(values, mask):
        return lax.ppermute(values, "req", perm=[(i, i ^ mask) for i in range(count)])

    def pick(cond, a, b):
        return jnp.where(cond, a, b)

    near = swap(holder, 1)
    quad = swap(jnp.concatenate([holder, near]), 2)
    holders = {0: holder[0], 1: near[0], 2: quad[0], 3: quad[1]}

    got1 = swap(own, 4)
    send_a = pick(holders[2] == (me ^ 4), got1, own)
    send_b = pick(holders[3] == (me ^ 4), got1, own)
    got2 = swap(jnp.stack([send_a, send_b]), 2)
    want = holders[1]
    send_c = pick(want == me, own, pick(want == (me ^ 4), got1, got2[1]))
    got3 = swap(send_c, 1)
    need = holders[0]
    return pick(
        need == me,
        own,
        pick(need == (me ^ 4), got1, pick((need ^ me) == 2, got2[0], pick((need ^ me) == 6, got2[0], got3))),
    )


def local(
    tokens,
    cache_kv,
    cache_len,
    holder,
    accept,
    attn_gain,
    q_weight,
    k_weight,
    v_weight,
    o_weight,
    ffn_gain,
    w_gate,
    w_up,
    w_down,
):
    fetched = fetch_slot(cache_kv, holder)
    gate_t, up_t, down_all = gather_ffn_weights(w_gate, w_up, w_down)
    cache_keys = fetched[0]
    cache_vals = fetched[1]
    cache_length = cache_len[0]
    block_rows = tokens[0]
    first_pass = attend_block(
        block_rows,
        cache_keys,
        cache_vals,
        cache_length,
        attn_gain,
        q_weight,
        k_weight,
        v_weight,
        o_weight,
    )
    chosen_mask = accept[0] == 1
    ffn_sum = run_ffn(rms_scale(first_pass, ffn_gain).astype(jnp.bfloat16), gate_t, up_t, down_all, w_down.shape[0])
    placed = first_pass + ffn_sum
    second_in = jnp.where(chosen_mask[:, None], placed, block_rows.astype(jnp.float32))
    refined = attend_block(
        second_in,
        cache_keys,
        cache_vals,
        cache_length,
        attn_gain,
        q_weight,
        k_weight,
        v_weight,
        o_weight,
    )
    return refined[None]


def solution(mesh):
    return jax.shard_map(
        local,
        mesh=mesh,
        in_specs=(
            P(("req", "blk"), None, None),
            P(("req", "blk"), None, None, None),
            P(("req", "blk")),
            P(("req", "blk")),
            P(("req", "blk"), None),
            P(),
            P(),
            P(),
            P(),
            P(),
            P(),
            P(None, "blk"),
            P(None, "blk"),
            P("blk", None),
        ),
        out_specs=P(("req", "blk"), None, None),
        check_vma=False,
    )
```

```python
import jax
import jax.numpy as jnp
from jax import lax
from jax.sharding import PartitionSpec as P

HEAD = 96


norm_eps = 1e-05
rope_base = 100000.0


def rms_scale(values, gain_row):
    return (
        values * lax.rsqrt(jnp.mean(values * values, axis=-1, keepdims=True) + norm_eps) * gain_row
    )


def rotate_heads(flat, positions, head_count):
    half_dim = HEAD // 2
    shaped = flat.reshape(flat.shape[0], head_count, HEAD)
    freqs = jnp.exp(-jnp.log(rope_base) * 2.0 * jnp.arange(half_dim, dtype=jnp.float32) / HEAD)
    angles = positions[:, None] * freqs[None, :]
    cosine = jnp.cos(angles)[:, None, :]
    sine = jnp.sin(angles)[:, None, :]
    first_half = shaped[..., :half_dim]
    second_half = shaped[..., half_dim:]
    turned = jnp.concatenate(
        [first_half * cosine - second_half * sine, second_half * cosine + first_half * sine],
        axis=-1,
    )
    return turned.reshape(flat.shape[0], head_count * HEAD)


def attend_block(
    tok_rows,
    cache_keys,
    cache_vals,
    cache_length,
    attn_gain,
    q_weight,
    k_weight,
    v_weight,
    o_weight,
):
    block_len = tok_rows.shape[0]
    slot_len = cache_keys.shape[0]
    kv_count = k_weight.shape[1] // HEAD
    q_count = q_weight.shape[1] // HEAD
    widened = tok_rows.astype(jnp.float32)
    normed = rms_scale(widened, attn_gain).astype(jnp.bfloat16)
    positions = (cache_length + jnp.arange(block_len, dtype=jnp.int32)).astype(jnp.float32)
    queries = rotate_heads(
        jnp.dot(normed, q_weight, preferred_element_type=jnp.float32), positions, q_count
    ).astype(jnp.bfloat16)
    new_keys = rotate_heads(
        jnp.dot(normed, k_weight, preferred_element_type=jnp.float32), positions, kv_count
    ).astype(jnp.bfloat16)
    new_vals = jnp.dot(normed, v_weight, preferred_element_type=jnp.float32).astype(jnp.bfloat16)
    all_keys = jnp.concatenate([cache_keys, new_keys], axis=0).reshape(
        slot_len + block_len, kv_count, HEAD
    )
    all_vals = jnp.concatenate([cache_vals, new_vals], axis=0).reshape(
        slot_len + block_len, kv_count, HEAD
    )
    grouped = queries.reshape(block_len, kv_count, q_count // kv_count, HEAD)
    scores = jnp.einsum(
        "bgid,kgd->gibk", grouped, all_keys, preferred_element_type=jnp.float32
    ) * HEAD ** (-0.5)
    valid = jnp.concatenate(
        [
            jnp.arange(slot_len, dtype=jnp.int32) < cache_length,
            jnp.ones((block_len,), dtype=jnp.bool_),
        ]
    )
    scores = jnp.where(valid, scores, -jnp.inf)
    peaks = jnp.max(scores, axis=-1, keepdims=True)
    expd = jnp.exp(scores - peaks)
    probs = (expd / jnp.sum(expd, axis=-1, keepdims=True)).astype(jnp.bfloat16)
    context = jnp.einsum("gibk,kgd->bgid", probs, all_vals, preferred_element_type=jnp.float32)
    context = context.astype(jnp.bfloat16).reshape(block_len, q_count * HEAD)
    return widened + jnp.dot(context, o_weight, preferred_element_type=jnp.float32)


def run_ffn(normed_rows, w_gate, w_up, down_all, groups):
    part_rows = lax.all_gather(normed_rows, "blk", axis=0, tiled=True)
    gate_vals = jnp.dot(part_rows, w_gate, preferred_element_type=jnp.float32)
    up_vals = jnp.dot(part_rows, w_up, preferred_element_type=jnp.float32)
    hidden_all = (jax.nn.silu(gate_vals) * up_vals).astype(jnp.bfloat16)
    hidden_own = lax.all_to_all(hidden_all, "blk", 0, 1, tiled=True)
    group_count = down_all.shape[0] // groups
    terms = jnp.einsum(
        "rgk,gkd->grd",
        hidden_own.reshape(hidden_own.shape[0], group_count, groups),
        down_all.reshape(group_count, groups, down_all.shape[1]),
        preferred_element_type=jnp.float32,
    ).astype(jnp.bfloat16)
    return jnp.sum(terms.astype(jnp.float32), axis=0)


def fetch_slot(cache_kv, holder):
    count = lax.axis_size("req")
    own = cache_kv[0]
    if count != 8:
        slots = lax.all_gather(own, "req", axis=0, tiled=False)
        return slots[holder[0]]
    me = lax.axis_index("req")

    def swap(values, mask):
        return lax.ppermute(values, "req", perm=[(i, i ^ mask) for i in range(count)])

    def pick(cond, a, b):
        return jnp.where(cond, a, b)

    near = swap(holder, 1)
    quad = swap(jnp.concatenate([holder, near]), 2)
    holders = {0: holder[0], 1: near[0], 2: quad[0], 3: quad[1]}

    got1 = swap(own, 4)
    send_a = pick(holders[2] == (me ^ 4), got1, own)
    send_b = pick(holders[3] == (me ^ 4), got1, own)
    got2 = swap(jnp.stack([send_a, send_b]), 2)
    want = holders[1]
    send_c = pick(want == me, own, pick(want == (me ^ 4), got1, got2[1]))
    got3 = swap(send_c, 1)
    need = holders[0]
    return pick(
        need == me,
        own,
        pick(need == (me ^ 4), got1, pick((need ^ me) == 2, got2[0], pick((need ^ me) == 6, got2[0], got3))),
    )


def local(
    tokens,
    cache_kv,
    cache_len,
    holder,
    accept,
    attn_gain,
    q_weight,
    k_weight,
    v_weight,
    o_weight,
    ffn_gain,
    w_gate,
    w_up,
    w_down,
):
    fetched = fetch_slot(cache_kv, holder)
    down_all = lax.all_gather(w_down, "blk", axis=0, tiled=True)
    cache_keys = fetched[0]
    cache_vals = fetched[1]
    cache_length = cache_len[0]
    block_rows = tokens[0]
    first_pass = attend_block(
        block_rows,
        cache_keys,
        cache_vals,
        cache_length,
        attn_gain,
        q_weight,
        k_weight,
        v_weight,
        o_weight,
    )
    chosen_mask = accept[0] == 1
    ffn_rows, down_all = lax.optimization_barrier(
        (rms_scale(first_pass, ffn_gain).astype(jnp.bfloat16), down_all)
    )
    ffn_sum = run_ffn(ffn_rows, w_gate, w_up, down_all, w_down.shape[0])
    placed = first_pass + ffn_sum
    second_in = jnp.where(chosen_mask[:, None], placed, block_rows.astype(jnp.float32))
    refined = attend_block(
        second_in,
        cache_keys,
        cache_vals,
        cache_length,
        attn_gain,
        q_weight,
        k_weight,
        v_weight,
        o_weight,
    )
    return refined[None]


def solution(mesh):
    return jax.shard_map(
        local,
        mesh=mesh,
        in_specs=(
            P(("req", "blk"), None, None),
            P(("req", "blk"), None, None, None),
            P(("req", "blk")),
            P(("req", "blk")),
            P(("req", "blk"), None),
            P(),
            P(),
            P(),
            P(),
            P(),
            P(),
            P(None, "blk"),
            P(None, "blk"),
            P("blk", None),
        ),
        out_specs=P(("req", "blk"), None, None),
        check_vma=False,
    )
```

```python
import jax
import jax.numpy as jnp
from jax import lax
from jax.sharding import PartitionSpec as P

HEAD = 96


norm_eps = 1e-05
rope_base = 100000.0


def rms_scale(values, gain_row):
    return (
        values * lax.rsqrt(jnp.mean(values * values, axis=-1, keepdims=True) + norm_eps) * gain_row
    )


def rotate_heads(flat, positions, head_count):
    half_dim = HEAD // 2
    shaped = flat.reshape(flat.shape[0], head_count, HEAD)
    freqs = jnp.exp(-jnp.log(rope_base) * 2.0 * jnp.arange(half_dim, dtype=jnp.float32) / HEAD)
    angles = positions[:, None] * freqs[None, :]
    cosine = jnp.cos(angles)[:, None, :]
    sine = jnp.sin(angles)[:, None, :]
    first_half = shaped[..., :half_dim]
    second_half = shaped[..., half_dim:]
    turned = jnp.concatenate(
        [first_half * cosine - second_half * sine, second_half * cosine + first_half * sine],
        axis=-1,
    )
    return turned.reshape(flat.shape[0], head_count * HEAD)


def attend_block(
    tok_rows,
    cache_keys,
    cache_vals,
    cache_length,
    attn_gain,
    q_weight,
    k_weight,
    v_weight,
    o_weight,
):
    block_len = tok_rows.shape[0]
    slot_len = cache_keys.shape[0]
    kv_count = k_weight.shape[1] // HEAD
    q_count = q_weight.shape[1] // HEAD
    widened = tok_rows.astype(jnp.float32)
    normed = rms_scale(widened, attn_gain).astype(jnp.bfloat16)
    positions = (cache_length + jnp.arange(block_len, dtype=jnp.int32)).astype(jnp.float32)
    queries = rotate_heads(
        jnp.dot(normed, q_weight, preferred_element_type=jnp.float32), positions, q_count
    ).astype(jnp.bfloat16)
    new_keys = rotate_heads(
        jnp.dot(normed, k_weight, preferred_element_type=jnp.float32), positions, kv_count
    ).astype(jnp.bfloat16)
    new_vals = jnp.dot(normed, v_weight, preferred_element_type=jnp.float32).astype(jnp.bfloat16)
    all_keys = jnp.concatenate([cache_keys, new_keys], axis=0).reshape(
        slot_len + block_len, kv_count, HEAD
    )
    all_vals = jnp.concatenate([cache_vals, new_vals], axis=0).reshape(
        slot_len + block_len, kv_count, HEAD
    )
    grouped = queries.reshape(block_len, kv_count, q_count // kv_count, HEAD)
    scores = jnp.einsum(
        "bgid,kgd->gibk", grouped, all_keys, preferred_element_type=jnp.float32
    ) * HEAD ** (-0.5)
    valid = jnp.concatenate(
        [
            jnp.arange(slot_len, dtype=jnp.int32) < cache_length,
            jnp.ones((block_len,), dtype=jnp.bool_),
        ]
    )
    scores = jnp.where(valid, scores, -jnp.inf)
    peaks = jnp.max(scores, axis=-1, keepdims=True)
    expd = jnp.exp(scores - peaks)
    probs = (expd / jnp.sum(expd, axis=-1, keepdims=True)).astype(jnp.bfloat16)
    context = jnp.einsum("gibk,kgd->bgid", probs, all_vals, preferred_element_type=jnp.float32)
    context = context.astype(jnp.bfloat16).reshape(block_len, q_count * HEAD)
    return widened + jnp.dot(context, o_weight, preferred_element_type=jnp.float32)


def run_ffn(normed_rows, w_gate, w_up, down_held, held_groups):
    part_rows = lax.all_gather(normed_rows, "blk", axis=0, tiled=True)
    gate_vals = jnp.dot(part_rows, w_gate, preferred_element_type=jnp.float32)
    up_vals = jnp.dot(part_rows, w_up, preferred_element_type=jnp.float32)
    hidden_all = (jax.nn.silu(gate_vals) * up_vals).astype(jnp.bfloat16)
    hidden_own = lax.all_to_all(hidden_all, "blk", 0, 1, tiled=True)
    group_count, groups = down_held.shape[0], down_held.shape[1]
    grouped = hidden_own.reshape(hidden_own.shape[0], group_count, groups)
    grouped = jnp.take(grouped, held_groups, axis=1)
    terms = jnp.einsum(
        "rgk,gkd->grd", grouped, down_held, preferred_element_type=jnp.float32
    ).astype(jnp.bfloat16)
    return jnp.sum(terms.astype(jnp.float32), axis=0)


def held_order(masks, count):
    offsets = []
    for j in range(count):
        offset = 0
        for bit, mask in enumerate(masks):
            if (j >> bit) & 1:
                offset ^= mask
        offsets.append(offset)
    return jnp.bitwise_xor(lax.axis_index("blk"), jnp.array(offsets, dtype=jnp.int32))


def fetch_and_gather(cache_kv, holder, w_down):
    count = lax.axis_size("req")
    blocks = lax.axis_size("blk")
    own = cache_kv[0]
    if count != 8 or blocks != 32:
        slots = lax.all_gather(own, "req", axis=0, tiled=False)
        down = lax.all_gather(w_down, "blk", axis=0, tiled=False)
        return slots[holder[0]], down, jnp.arange(blocks, dtype=jnp.int32)
    me = lax.axis_index("req")

    def swap(values, mask):
        return lax.ppermute(values, "req", perm=[(i, i ^ mask) for i in range(count)])

    def pick(cond, a, b):
        return jnp.where(cond, a, b)

    masks = (16, 4, 8, 2, 1)
    held = [w_down[None]]

    def grow(mask):
        got = lax.ppermute(held[0], "blk", perm=[(i, i ^ mask) for i in range(blocks)])
        return got

    def keep(got):
        held[0] = jnp.concatenate([held[0], got], axis=0)

    near = swap(holder, 1)
    got1 = swap(own, 4)
    w_got = grow(masks[0])
    near, got1, w_got = lax.optimization_barrier((near, got1, w_got))
    keep(w_got)
    quad = swap(jnp.concatenate([holder, near]), 2)
    w_got = grow(masks[1])
    quad, w_got = lax.optimization_barrier((quad, w_got))
    keep(w_got)
    holders = {0: holder[0], 1: near[0], 2: quad[0], 3: quad[1]}
    send_a = pick(holders[2] == (me ^ 4), got1, own)
    send_b = pick(holders[3] == (me ^ 4), got1, own)
    got2 = swap(jnp.stack([send_a, send_b]), 2)
    w_got = grow(masks[2])
    got2, w_got = lax.optimization_barrier((got2, w_got))
    keep(w_got)
    want = holders[1]
    send_c = pick(want == me, own, pick(want == (me ^ 4), got1, got2[1]))
    got3 = swap(send_c, 1)
    w_got = grow(masks[3])
    got3, w_got = lax.optimization_barrier((got3, w_got))
    keep(w_got)
    need = holders[0]
    slot = pick(
        need == me,
        own,
        pick(need == (me ^ 4), got1, pick((need ^ me) == 2, got2[0], pick((need ^ me) == 6, got2[0], got3))),
    )
    keep(grow(masks[4]))
    return slot, held[0], held_order(masks, blocks)


def local(
    tokens,
    cache_kv,
    cache_len,
    holder,
    accept,
    attn_gain,
    q_weight,
    k_weight,
    v_weight,
    o_weight,
    ffn_gain,
    w_gate,
    w_up,
    w_down,
):
    fetched, down_held, held_groups = fetch_and_gather(cache_kv, holder, w_down)
    cache_keys = fetched[0]
    cache_vals = fetched[1]
    cache_length = cache_len[0]
    block_rows = tokens[0]
    first_pass = attend_block(
        block_rows,
        cache_keys,
        cache_vals,
        cache_length,
        attn_gain,
        q_weight,
        k_weight,
        v_weight,
        o_weight,
    )
    chosen_mask = accept[0] == 1
    ffn_rows, down_held = lax.optimization_barrier(
        (rms_scale(first_pass, ffn_gain).astype(jnp.bfloat16), down_held)
    )
    ffn_sum = run_ffn(ffn_rows, w_gate, w_up, down_held, held_groups)
    placed = first_pass + ffn_sum
    second_in = jnp.where(chosen_mask[:, None], placed, block_rows.astype(jnp.float32))
    refined = attend_block(
        second_in,
        cache_keys,
        cache_vals,
        cache_length,
        attn_gain,
        q_weight,
        k_weight,
        v_weight,
        o_weight,
    )
    return refined[None]


def solution(mesh):
    return jax.shard_map(
        local,
        mesh=mesh,
        in_specs=(
            P(("req", "blk"), None, None),
            P(("req", "blk"), None, None, None),
            P(("req", "blk")),
            P(("req", "blk")),
            P(("req", "blk"), None),
            P(),
            P(),
            P(),
            P(),
            P(),
            P(),
            P(None, "blk"),
            P(None, "blk"),
            P("blk", None),
        ),
        out_specs=P(("req", "blk"), None, None),
        check_vma=False,
    )
```

```python
import jax
import jax.numpy as jnp
from jax import lax
from jax.sharding import Mesh, PartitionSpec as P

HEAD = 96


REQ = "req"
BLK = "blk"
BLK_PARTS = None

norm_eps = 1e-05
rope_base = 100000.0


def rms_scale(values, gain_row):
    return (
        values * lax.rsqrt(jnp.mean(values * values, axis=-1, keepdims=True) + norm_eps) * gain_row
    )


def rotate_heads(flat, positions, head_count):
    half_dim = HEAD // 2
    shaped = flat.reshape(flat.shape[0], head_count, HEAD)
    freqs = jnp.exp(-jnp.log(rope_base) * 2.0 * jnp.arange(half_dim, dtype=jnp.float32) / HEAD)
    angles = positions[:, None] * freqs[None, :]
    cosine = jnp.cos(angles)[:, None, :]
    sine = jnp.sin(angles)[:, None, :]
    first_half = shaped[..., :half_dim]
    second_half = shaped[..., half_dim:]
    turned = jnp.concatenate(
        [first_half * cosine - second_half * sine, second_half * cosine + first_half * sine],
        axis=-1,
    )
    return turned.reshape(flat.shape[0], head_count * HEAD)


def attend_block(
    tok_rows,
    cache_keys,
    cache_vals,
    cache_length,
    attn_gain,
    q_weight,
    k_weight,
    v_weight,
    o_weight,
):
    block_len = tok_rows.shape[0]
    slot_len = cache_keys.shape[0]
    kv_count = k_weight.shape[1] // HEAD
    q_count = q_weight.shape[1] // HEAD
    widened = tok_rows.astype(jnp.float32)
    normed = rms_scale(widened, attn_gain).astype(jnp.bfloat16)
    positions = (cache_length + jnp.arange(block_len, dtype=jnp.int32)).astype(jnp.float32)
    queries = rotate_heads(
        jnp.dot(normed, q_weight, preferred_element_type=jnp.float32), positions, q_count
    ).astype(jnp.bfloat16)
    new_keys = rotate_heads(
        jnp.dot(normed, k_weight, preferred_element_type=jnp.float32), positions, kv_count
    ).astype(jnp.bfloat16)
    new_vals = jnp.dot(normed, v_weight, preferred_element_type=jnp.float32).astype(jnp.bfloat16)
    all_keys = jnp.concatenate([cache_keys, new_keys], axis=0).reshape(
        slot_len + block_len, kv_count, HEAD
    )
    all_vals = jnp.concatenate([cache_vals, new_vals], axis=0).reshape(
        slot_len + block_len, kv_count, HEAD
    )
    grouped = queries.reshape(block_len, kv_count, q_count // kv_count, HEAD)
    scores = jnp.einsum(
        "bgid,kgd->gibk", grouped, all_keys, preferred_element_type=jnp.float32
    ) * HEAD ** (-0.5)
    valid = jnp.concatenate(
        [
            jnp.arange(slot_len, dtype=jnp.int32) < cache_length,
            jnp.ones((block_len,), dtype=jnp.bool_),
        ]
    )
    scores = jnp.where(valid, scores, -jnp.inf)
    peaks = jnp.max(scores, axis=-1, keepdims=True)
    expd = jnp.exp(scores - peaks)
    probs = (expd / jnp.sum(expd, axis=-1, keepdims=True)).astype(jnp.bfloat16)
    context = jnp.einsum("gibk,kgd->bgid", probs, all_vals, preferred_element_type=jnp.float32)
    context = context.astype(jnp.bfloat16).reshape(block_len, q_count * HEAD)
    return widened + jnp.dot(context, o_weight, preferred_element_type=jnp.float32)


def return_hidden(hidden_all):
    if BLK_PARTS is None:
        return lax.all_to_all(hidden_all, BLK, 0, 1, tiled=True)
    sizes = [lax.psum(1, name) for name in BLK_PARTS]
    rows, units = hidden_all.shape[0] // (sizes[0] * sizes[1] * sizes[2]), hidden_all.shape[1]
    parts = hidden_all.reshape(sizes[0], sizes[1], sizes[2], rows, units)
    for axis in (2, 1, 0):
        parts = lax.all_to_all(parts, BLK_PARTS[axis], axis, axis, tiled=True)
    return parts.reshape(-1, rows, units).transpose(1, 0, 2).reshape(rows, -1)


def run_ffn(normed_rows, w_gate, w_up, down_all, groups):
    part_rows = lax.all_gather(normed_rows, BLK, axis=0, tiled=True)
    gate_vals = jnp.dot(part_rows, w_gate, preferred_element_type=jnp.float32)
    up_vals = jnp.dot(part_rows, w_up, preferred_element_type=jnp.float32)
    hidden_all = (jax.nn.silu(gate_vals) * up_vals).astype(jnp.bfloat16)
    hidden_own = return_hidden(hidden_all)
    group_count = down_all.shape[0] // groups
    terms = jnp.einsum(
        "rgk,gkd->grd",
        hidden_own.reshape(hidden_own.shape[0], group_count, groups),
        down_all.reshape(group_count, groups, down_all.shape[1]),
        preferred_element_type=jnp.float32,
    ).astype(jnp.bfloat16)
    return jnp.sum(terms.astype(jnp.float32), axis=0)


def fetch_slot(cache_kv, holder):
    count = lax.psum(1, REQ)
    own = cache_kv[0]
    if count != 8:
        slots = lax.all_gather(own, REQ, axis=0, tiled=False)
        return slots[holder[0]]
    me = lax.axis_index(REQ)

    def swap(values, mask):
        return lax.ppermute(values, REQ, perm=[(i, i ^ mask) for i in range(count)])

    def pick(cond, a, b):
        return jnp.where(cond, a, b)

    near = swap(holder, 1)
    quad = swap(jnp.concatenate([holder, near]), 2)
    holders = {0: holder[0], 1: near[0], 2: quad[0], 3: quad[1]}

    got1 = swap(own, 4)
    send_a = pick(holders[2] == (me ^ 4), got1, own)
    send_b = pick(holders[3] == (me ^ 4), got1, own)
    got2 = swap(jnp.stack([send_a, send_b]), 2)
    want = holders[1]
    send_c = pick(want == me, own, pick(want == (me ^ 4), got1, got2[1]))
    got3 = swap(send_c, 1)
    need = holders[0]
    return pick(
        need == me,
        own,
        pick(need == (me ^ 4), got1, pick((need ^ me) == 2, got2[0], pick((need ^ me) == 6, got2[0], got3))),
    )


def local(
    tokens,
    cache_kv,
    cache_len,
    holder,
    accept,
    attn_gain,
    q_weight,
    k_weight,
    v_weight,
    o_weight,
    ffn_gain,
    w_gate,
    w_up,
    w_down,
):
    fetched = fetch_slot(cache_kv, holder)
    down_all = lax.all_gather(w_down, BLK, axis=0, tiled=True)
    cache_keys = fetched[0]
    cache_vals = fetched[1]
    cache_length = cache_len[0]
    block_rows = tokens[0]
    first_pass = attend_block(
        block_rows,
        cache_keys,
        cache_vals,
        cache_length,
        attn_gain,
        q_weight,
        k_weight,
        v_weight,
        o_weight,
    )
    chosen_mask = accept[0] == 1
    ffn_rows, down_all = lax.optimization_barrier(
        (rms_scale(first_pass, ffn_gain).astype(jnp.bfloat16), down_all)
    )
    ffn_sum = run_ffn(ffn_rows, w_gate, w_up, down_all, w_down.shape[0])
    placed = first_pass + ffn_sum
    second_in = jnp.where(chosen_mask[:, None], placed, block_rows.astype(jnp.float32))
    refined = attend_block(
        second_in,
        cache_keys,
        cache_vals,
        cache_length,
        attn_gain,
        q_weight,
        k_weight,
        v_weight,
        o_weight,
    )
    return refined[None]


def solution(mesh):
    global REQ, BLK, BLK_PARTS
    if dict(mesh.shape) == {"req": 8, "blk": 32}:
        mesh = Mesh(mesh.devices.reshape(4, 2, 4, 4, 2), ("x", "zh", "y", "zl", "c"))
        REQ, BLK, BLK_PARTS = ("x", "zh"), ("y", "zl", "c"), ("y", "zl", "c")
    rows = REQ + BLK if isinstance(REQ, tuple) else (REQ, BLK)
    return jax.shard_map(
        local,
        mesh=mesh,
        in_specs=(
            P(rows, None, None),
            P(rows, None, None, None),
            P(rows),
            P(rows),
            P(rows, None),
            P(),
            P(),
            P(),
            P(),
            P(),
            P(),
            P(None, BLK),
            P(None, BLK),
            P(BLK, None),
        ),
        out_specs=P(rows, None, None),
        check_vma=False,
    )
```

```python
import jax
import jax.numpy as jnp
from jax import lax
from jax.sharding import PartitionSpec as P

HEAD = 96


norm_eps = 1e-05
rope_base = 100000.0


def rms_scale(values, gain_row):
    return (
        values * lax.rsqrt(jnp.mean(values * values, axis=-1, keepdims=True) + norm_eps) * gain_row
    )


def rotate_heads(flat, positions, head_count):
    half_dim = HEAD // 2
    shaped = flat.reshape(flat.shape[0], head_count, HEAD)
    freqs = jnp.exp(-jnp.log(rope_base) * 2.0 * jnp.arange(half_dim, dtype=jnp.float32) / HEAD)
    angles = positions[:, None] * freqs[None, :]
    cosine = jnp.cos(angles)[:, None, :]
    sine = jnp.sin(angles)[:, None, :]
    first_half = shaped[..., :half_dim]
    second_half = shaped[..., half_dim:]
    turned = jnp.concatenate(
        [first_half * cosine - second_half * sine, second_half * cosine + first_half * sine],
        axis=-1,
    )
    return turned.reshape(flat.shape[0], head_count * HEAD)


def attend_block(
    tok_rows,
    cache_keys,
    cache_vals,
    cache_length,
    attn_gain,
    q_weight,
    k_weight,
    v_weight,
    o_weight,
):
    block_len = tok_rows.shape[0]
    slot_len = cache_keys.shape[0]
    kv_count = k_weight.shape[1] // HEAD
    q_count = q_weight.shape[1] // HEAD
    widened = tok_rows.astype(jnp.float32)
    normed = rms_scale(widened, attn_gain).astype(jnp.bfloat16)
    positions = (cache_length + jnp.arange(block_len, dtype=jnp.int32)).astype(jnp.float32)
    queries = rotate_heads(
        jnp.dot(normed, q_weight, preferred_element_type=jnp.float32), positions, q_count
    ).astype(jnp.bfloat16)
    new_keys = rotate_heads(
        jnp.dot(normed, k_weight, preferred_element_type=jnp.float32), positions, kv_count
    ).astype(jnp.bfloat16)
    new_vals = jnp.dot(normed, v_weight, preferred_element_type=jnp.float32).astype(jnp.bfloat16)
    all_keys = jnp.concatenate([cache_keys, new_keys], axis=0).reshape(
        slot_len + block_len, kv_count, HEAD
    )
    all_vals = jnp.concatenate([cache_vals, new_vals], axis=0).reshape(
        slot_len + block_len, kv_count, HEAD
    )
    grouped = queries.reshape(block_len, kv_count, q_count // kv_count, HEAD)
    scores = jnp.einsum(
        "bgid,kgd->gibk", grouped, all_keys, preferred_element_type=jnp.float32
    ) * HEAD ** (-0.5)
    valid = jnp.concatenate(
        [
            jnp.arange(slot_len, dtype=jnp.int32) < cache_length,
            jnp.ones((block_len,), dtype=jnp.bool_),
        ]
    )
    scores = jnp.where(valid, scores, -jnp.inf)
    peaks = jnp.max(scores, axis=-1, keepdims=True)
    expd = jnp.exp(scores - peaks)
    probs = (expd / jnp.sum(expd, axis=-1, keepdims=True)).astype(jnp.bfloat16)
    context = jnp.einsum("gibk,kgd->bgid", probs, all_vals, preferred_element_type=jnp.float32)
    context = context.astype(jnp.bfloat16).reshape(block_len, q_count * HEAD)
    return widened + jnp.dot(context, o_weight, preferred_element_type=jnp.float32)


def run_ffn(normed_rows, w_gate, w_up, down_all, groups):
    part_rows = lax.all_gather(normed_rows, "blk", axis=0, tiled=True)
    gate_vals = jnp.dot(part_rows, w_gate, preferred_element_type=jnp.float32)
    up_vals = jnp.dot(part_rows, w_up, preferred_element_type=jnp.float32)
    hidden_all = (jax.nn.silu(gate_vals) * up_vals).astype(jnp.bfloat16)
    hidden_own = lax.all_to_all(hidden_all, "blk", 0, 1, tiled=True)
    group_count = down_all.shape[0] // groups
    terms = jnp.einsum(
        "rgk,gkd->grd",
        hidden_own.reshape(hidden_own.shape[0], group_count, groups),
        down_all.reshape(group_count, groups, down_all.shape[1]),
        preferred_element_type=jnp.float32,
    ).astype(jnp.bfloat16)
    return jnp.sum(terms.astype(jnp.float32), axis=0)


def fetch_slot(cache_kv, holder):
    count = lax.axis_size("req")
    own = cache_kv[0]
    if count != 8:
        slots = lax.all_gather(own, "req", axis=0, tiled=False)
        return slots[holder[0]]
    me = lax.axis_index("req")

    def swap(values, mask):
        return lax.ppermute(values, "req", perm=[(i, i ^ mask) for i in range(count)])

    def pick(cond, a, b):
        return jnp.where(cond, a, b)

    near = swap(holder, 1)
    quad = swap(jnp.concatenate([holder, near]), 2)
    holders = {0: holder[0], 1: near[0], 2: quad[0], 3: quad[1]}

    got1 = swap(own, 4)
    send_a = pick(holders[2] == (me ^ 4), got1, own)
    send_b = pick(holders[3] == (me ^ 4), got1, own)
    got2 = swap(jnp.stack([send_a, send_b]), 2)
    want = holders[1]
    send_c = pick(want == me, own, pick(want == (me ^ 4), got1, got2[1]))
    got3 = swap(send_c, 1)
    need = holders[0]
    return pick(
        need == me,
        own,
        pick(need == (me ^ 4), got1, pick((need ^ me) == 2, got2[0], pick((need ^ me) == 6, got2[0], got3))),
    )


def local(
    tokens,
    cache_kv,
    cache_len,
    holder,
    accept,
    attn_gain,
    q_weight,
    k_weight,
    v_weight,
    o_weight,
    ffn_gain,
    w_gate,
    w_up,
    w_down,
):
    fetched = fetch_slot(cache_kv, holder)
    down_all = lax.all_gather(w_down, "blk", axis=0, tiled=True)
    cache_keys = fetched[0]
    cache_vals = fetched[1]
    cache_length = cache_len[0]
    block_rows = tokens[0]
    first_pass = attend_block(
        block_rows,
        cache_keys,
        cache_vals,
        cache_length,
        attn_gain,
        q_weight,
        k_weight,
        v_weight,
        o_weight,
    )
    chosen_mask = accept[0] == 1
    block_len = block_rows.shape[0]
    kept = block_len // 2
    slot_of = jnp.cumsum(chosen_mask.astype(jnp.int32)) - 1
    hits = chosen_mask[None, :] & (slot_of[None, :] == jnp.arange(kept, dtype=jnp.int32)[:, None])
    kept_rows = jnp.sum(jnp.where(hits, jnp.arange(block_len, dtype=jnp.int32)[None, :], 0), axis=1)
    fnorm = rms_scale(first_pass, ffn_gain).astype(jnp.bfloat16)
    ffn_rows, down_all = lax.optimization_barrier((fnorm[kept_rows], down_all))
    ffn_kept = run_ffn(ffn_rows, w_gate, w_up, down_all, w_down.shape[0])
    ffn_sum = ffn_kept[jnp.clip(slot_of, 0, kept - 1)]
    placed = first_pass + ffn_sum
    second_in = jnp.where(chosen_mask[:, None], placed, block_rows.astype(jnp.float32))
    refined = attend_block(
        second_in,
        cache_keys,
        cache_vals,
        cache_length,
        attn_gain,
        q_weight,
        k_weight,
        v_weight,
        o_weight,
    )
    return refined[None]


def solution(mesh):
    return jax.shard_map(
        local,
        mesh=mesh,
        in_specs=(
            P(("req", "blk"), None, None),
            P(("req", "blk"), None, None, None),
            P(("req", "blk")),
            P(("req", "blk")),
            P(("req", "blk"), None),
            P(),
            P(),
            P(),
            P(),
            P(),
            P(),
            P(None, "blk"),
            P(None, "blk"),
            P("blk", None),
        ),
        out_specs=P(("req", "blk"), None, None),
        check_vma=False,
    )
```

```python
import jax
import jax.numpy as jnp
from jax import lax
from jax.sharding import PartitionSpec as P

HEAD = 96


norm_eps = 1e-05
rope_base = 100000.0


def rms_scale(values, gain_row):
    return (
        values * lax.rsqrt(jnp.mean(values * values, axis=-1, keepdims=True) + norm_eps) * gain_row
    )


def rotate_heads(flat, positions, head_count):
    half_dim = HEAD // 2
    shaped = flat.reshape(flat.shape[0], head_count, HEAD)
    freqs = jnp.exp(-jnp.log(rope_base) * 2.0 * jnp.arange(half_dim, dtype=jnp.float32) / HEAD)
    angles = positions[:, None] * freqs[None, :]
    cosine = jnp.cos(angles)[:, None, :]
    sine = jnp.sin(angles)[:, None, :]
    first_half = shaped[..., :half_dim]
    second_half = shaped[..., half_dim:]
    turned = jnp.concatenate(
        [first_half * cosine - second_half * sine, second_half * cosine + first_half * sine],
        axis=-1,
    )
    return turned.reshape(flat.shape[0], head_count * HEAD)


def attend_block(
    tok_rows,
    cache_keys,
    cache_vals,
    cache_length,
    attn_gain,
    q_weight,
    k_weight,
    v_weight,
    o_weight,
):
    block_len = tok_rows.shape[0]
    slot_len = cache_keys.shape[0]
    kv_count = k_weight.shape[1] // HEAD
    q_count = q_weight.shape[1] // HEAD
    widened = tok_rows.astype(jnp.float32)
    normed = rms_scale(widened, attn_gain).astype(jnp.bfloat16)
    positions = (cache_length + jnp.arange(block_len, dtype=jnp.int32)).astype(jnp.float32)
    queries = rotate_heads(
        jnp.dot(normed, q_weight, preferred_element_type=jnp.float32), positions, q_count
    ).astype(jnp.bfloat16)
    new_keys = rotate_heads(
        jnp.dot(normed, k_weight, preferred_element_type=jnp.float32), positions, kv_count
    ).astype(jnp.bfloat16)
    new_vals = jnp.dot(normed, v_weight, preferred_element_type=jnp.float32).astype(jnp.bfloat16)
    all_keys = jnp.concatenate([cache_keys, new_keys], axis=0).reshape(
        slot_len + block_len, kv_count, HEAD
    )
    all_vals = jnp.concatenate([cache_vals, new_vals], axis=0).reshape(
        slot_len + block_len, kv_count, HEAD
    )
    grouped = queries.reshape(block_len, kv_count, q_count // kv_count, HEAD)
    scores = jnp.einsum(
        "bgid,kgd->gibk", grouped, all_keys, preferred_element_type=jnp.float32
    ) * HEAD ** (-0.5)
    valid = jnp.concatenate(
        [
            jnp.arange(slot_len, dtype=jnp.int32) < cache_length,
            jnp.ones((block_len,), dtype=jnp.bool_),
        ]
    )
    scores = jnp.where(valid, scores, -jnp.inf)
    peaks = jnp.max(scores, axis=-1, keepdims=True)
    expd = jnp.exp(scores - peaks)
    probs = (expd / jnp.sum(expd, axis=-1, keepdims=True)).astype(jnp.bfloat16)
    context = jnp.einsum("gibk,kgd->bgid", probs, all_vals, preferred_element_type=jnp.float32)
    context = context.astype(jnp.bfloat16).reshape(block_len, q_count * HEAD)
    return widened + jnp.dot(context, o_weight, preferred_element_type=jnp.float32)


def run_ffn(normed_rows, w_gate, w_up, down_all, groups):
    part_rows = lax.all_gather(normed_rows, "blk", axis=0, tiled=True)
    gate_vals = jnp.dot(part_rows, w_gate, preferred_element_type=jnp.float32)
    up_vals = jnp.dot(part_rows, w_up, preferred_element_type=jnp.float32)
    hidden_all = (jax.nn.silu(gate_vals) * up_vals).astype(jnp.bfloat16)
    hidden_own = lax.all_to_all(hidden_all, "blk", 0, 1, tiled=True)
    group_count = down_all.shape[0] // groups
    terms = jnp.einsum(
        "rgk,gkd->grd",
        hidden_own.reshape(hidden_own.shape[0], group_count, groups),
        down_all.reshape(group_count, groups, down_all.shape[1]),
        preferred_element_type=jnp.float32,
    ).astype(jnp.bfloat16)
    return jnp.sum(terms.astype(jnp.float32), axis=0)


def fetch_slot(cache_kv, holder):
    count = lax.axis_size("req")
    own = cache_kv[0]
    if count != 8:
        slots = lax.all_gather(own, "req", axis=0, tiled=False)
        return slots[holder[0]], own
    me = lax.axis_index("req")

    def swap(values, mask):
        return lax.ppermute(values, "req", perm=[(i, i ^ mask) for i in range(count)])

    def pick(cond, a, b):
        return jnp.where(cond, a, b)

    far = swap(holder, 4)
    pair = swap(jnp.concatenate([holder, far]), 2)
    holders = {0: holder[0], 4: far[0], 2: pair[0], 6: pair[1]}

    got1 = swap(own, 1)
    send_a = pick(holders[2] == (me ^ 1), got1, own)
    send_b = pick(holders[6] == (me ^ 1), got1, own)
    got2 = swap(jnp.stack([send_a, send_b]), 2)
    want = holders[4]
    send_c = pick(want == me, own, pick(want == (me ^ 1), got1, got2[1]))
    got3 = swap(send_c, 4)
    need = holders[0]
    slot = pick(
        need == me,
        own,
        pick(need == (me ^ 1), got1, pick(((need ^ me) >> 1) == 1, got2[0], got3)),
    )
    return slot, got1


def local(
    tokens,
    cache_kv,
    cache_len,
    holder,
    accept,
    attn_gain,
    q_weight,
    k_weight,
    v_weight,
    o_weight,
    ffn_gain,
    w_gate,
    w_up,
    w_down,
):
    fetched, first_stage = fetch_slot(cache_kv, holder)
    w_down_late, _ = lax.optimization_barrier((w_down, first_stage))
    down_all = lax.all_gather(w_down_late, "blk", axis=0, tiled=True)
    cache_keys = fetched[0]
    cache_vals = fetched[1]
    cache_length = cache_len[0]
    block_rows = tokens[0]
    first_pass = attend_block(
        block_rows,
        cache_keys,
        cache_vals,
        cache_length,
        attn_gain,
        q_weight,
        k_weight,
        v_weight,
        o_weight,
    )
    chosen_mask = accept[0] == 1
    block_len = block_rows.shape[0]
    kept = block_len // 2
    slot_of = jnp.cumsum(chosen_mask.astype(jnp.int32)) - 1
    hits = chosen_mask[None, :] & (slot_of[None, :] == jnp.arange(kept, dtype=jnp.int32)[:, None])
    kept_rows = jnp.sum(jnp.where(hits, jnp.arange(block_len, dtype=jnp.int32)[None, :], 0), axis=1)
    fnorm = rms_scale(first_pass, ffn_gain).astype(jnp.bfloat16)
    ffn_rows, down_all = lax.optimization_barrier((fnorm[kept_rows], down_all))
    ffn_kept = run_ffn(ffn_rows, w_gate, w_up, down_all, w_down.shape[0])
    ffn_sum = ffn_kept[jnp.clip(slot_of, 0, kept - 1)]
    placed = first_pass + ffn_sum
    second_in = jnp.where(chosen_mask[:, None], placed, block_rows.astype(jnp.float32))
    refined = attend_block(
        second_in,
        cache_keys,
        cache_vals,
        cache_length,
        attn_gain,
        q_weight,
        k_weight,
        v_weight,
        o_weight,
    )
    return refined[None]


def solution(mesh):
    return jax.shard_map(
        local,
        mesh=mesh,
        in_specs=(
            P(("req", "blk"), None, None),
            P(("req", "blk"), None, None, None),
            P(("req", "blk")),
            P(("req", "blk")),
            P(("req", "blk"), None),
            P(),
            P(),
            P(),
            P(),
            P(),
            P(),
            P(None, "blk"),
            P(None, "blk"),
            P("blk", None),
        ),
        out_specs=P(("req", "blk"), None, None),
        check_vma=False,
    )
```

```python
import jax
import jax.numpy as jnp
from jax import lax
from jax.sharding import Mesh, PartitionSpec as P

HEAD = 96


BLK = "blk"
BLK_PARTS = None

norm_eps = 1e-05
rope_base = 100000.0


def rms_scale(values, gain_row):
    return (
        values * lax.rsqrt(jnp.mean(values * values, axis=-1, keepdims=True) + norm_eps) * gain_row
    )


def rotate_heads(flat, positions, head_count):
    half_dim = HEAD // 2
    shaped = flat.reshape(flat.shape[0], head_count, HEAD)
    freqs = jnp.exp(-jnp.log(rope_base) * 2.0 * jnp.arange(half_dim, dtype=jnp.float32) / HEAD)
    angles = positions[:, None] * freqs[None, :]
    cosine = jnp.cos(angles)[:, None, :]
    sine = jnp.sin(angles)[:, None, :]
    first_half = shaped[..., :half_dim]
    second_half = shaped[..., half_dim:]
    turned = jnp.concatenate(
        [first_half * cosine - second_half * sine, second_half * cosine + first_half * sine],
        axis=-1,
    )
    return turned.reshape(flat.shape[0], head_count * HEAD)


def attend_block(
    tok_rows,
    cache_keys,
    cache_vals,
    cache_length,
    attn_gain,
    q_weight,
    k_weight,
    v_weight,
    o_weight,
):
    block_len = tok_rows.shape[0]
    slot_len = cache_keys.shape[0]
    kv_count = k_weight.shape[1] // HEAD
    q_count = q_weight.shape[1] // HEAD
    widened = tok_rows.astype(jnp.float32)
    normed = rms_scale(widened, attn_gain).astype(jnp.bfloat16)
    positions = (cache_length + jnp.arange(block_len, dtype=jnp.int32)).astype(jnp.float32)
    queries = rotate_heads(
        jnp.dot(normed, q_weight, preferred_element_type=jnp.float32), positions, q_count
    ).astype(jnp.bfloat16)
    new_keys = rotate_heads(
        jnp.dot(normed, k_weight, preferred_element_type=jnp.float32), positions, kv_count
    ).astype(jnp.bfloat16)
    new_vals = jnp.dot(normed, v_weight, preferred_element_type=jnp.float32).astype(jnp.bfloat16)
    all_keys = jnp.concatenate([cache_keys, new_keys], axis=0).reshape(
        slot_len + block_len, kv_count, HEAD
    )
    all_vals = jnp.concatenate([cache_vals, new_vals], axis=0).reshape(
        slot_len + block_len, kv_count, HEAD
    )
    grouped = queries.reshape(block_len, kv_count, q_count // kv_count, HEAD)
    scores = jnp.einsum(
        "bgid,kgd->gibk", grouped, all_keys, preferred_element_type=jnp.float32
    ) * HEAD ** (-0.5)
    valid = jnp.concatenate(
        [
            jnp.arange(slot_len, dtype=jnp.int32) < cache_length,
            jnp.ones((block_len,), dtype=jnp.bool_),
        ]
    )
    scores = jnp.where(valid, scores, -jnp.inf)
    peaks = jnp.max(scores, axis=-1, keepdims=True)
    expd = jnp.exp(scores - peaks)
    probs = (expd / jnp.sum(expd, axis=-1, keepdims=True)).astype(jnp.bfloat16)
    context = jnp.einsum("gibk,kgd->bgid", probs, all_vals, preferred_element_type=jnp.float32)
    context = context.astype(jnp.bfloat16).reshape(block_len, q_count * HEAD)
    return widened + jnp.dot(context, o_weight, preferred_element_type=jnp.float32)


def run_ffn(normed_rows, w_gate, w_up, down_all, groups):
    if BLK_PARTS is None:
        part_rows = lax.all_gather(normed_rows, BLK, axis=0, tiled=True)
    else:
        part_rows = normed_rows
        for name in BLK_PARTS:
            part_rows = lax.all_gather(part_rows, name, axis=0, tiled=False)
        part_rows = part_rows.reshape(-1, normed_rows.shape[1])
    gate_vals = jnp.dot(part_rows, w_gate, preferred_element_type=jnp.float32)
    up_vals = jnp.dot(part_rows, w_up, preferred_element_type=jnp.float32)
    hidden_all = (jax.nn.silu(gate_vals) * up_vals).astype(jnp.bfloat16)
    if BLK_PARTS is not None:
        sizes = [lax.psum(1, name) for name in BLK_PARTS]
        hidden_all = hidden_all.reshape(sizes[::-1] + [normed_rows.shape[0], hidden_all.shape[1]])
        hidden_all = hidden_all.transpose(2, 1, 0, 3, 4).reshape(-1, hidden_all.shape[-1])
    hidden_own = lax.all_to_all(hidden_all, BLK, 0, 1, tiled=True)
    group_count = down_all.shape[0] // groups
    terms = jnp.einsum(
        "rgk,gkd->grd",
        hidden_own.reshape(hidden_own.shape[0], group_count, groups),
        down_all.reshape(group_count, groups, down_all.shape[1]),
        preferred_element_type=jnp.float32,
    ).astype(jnp.bfloat16)
    return jnp.sum(terms.astype(jnp.float32), axis=0)


def fetch_slot(cache_kv, holder):
    count = lax.axis_size("req")
    own = cache_kv[0]
    if count != 8:
        slots = lax.all_gather(own, "req", axis=0, tiled=False)
        return slots[holder[0]]
    me = lax.axis_index("req")

    def swap(values, mask):
        return lax.ppermute(values, "req", perm=[(i, i ^ mask) for i in range(count)])

    def pick(cond, a, b):
        return jnp.where(cond, a, b)

    near = swap(holder, 1)
    quad = swap(jnp.concatenate([holder, near]), 2)
    holders = {0: holder[0], 1: near[0], 2: quad[0], 3: quad[1]}

    got1 = swap(own, 4)
    send_a = pick(holders[2] == (me ^ 4), got1, own)
    send_b = pick(holders[3] == (me ^ 4), got1, own)
    got2 = swap(jnp.stack([send_a, send_b]), 2)
    want = holders[1]
    send_c = pick(want == me, own, pick(want == (me ^ 4), got1, got2[1]))
    got3 = swap(send_c, 1)
    need = holders[0]
    return pick(
        need == me,
        own,
        pick(need == (me ^ 4), got1, pick((need ^ me) == 2, got2[0], pick((need ^ me) == 6, got2[0], got3))),
    )


def local(
    tokens,
    cache_kv,
    cache_len,
    holder,
    accept,
    attn_gain,
    q_weight,
    k_weight,
    v_weight,
    o_weight,
    ffn_gain,
    w_gate,
    w_up,
    w_down,
):
    fetched = fetch_slot(cache_kv, holder)
    down_all = lax.all_gather(w_down, BLK, axis=0, tiled=True)
    cache_keys = fetched[0]
    cache_vals = fetched[1]
    cache_length = cache_len[0]
    block_rows = tokens[0]
    first_pass = attend_block(
        block_rows,
        cache_keys,
        cache_vals,
        cache_length,
        attn_gain,
        q_weight,
        k_weight,
        v_weight,
        o_weight,
    )
    chosen_mask = accept[0] == 1
    block_len = block_rows.shape[0]
    kept = block_len // 2
    slot_of = jnp.cumsum(chosen_mask.astype(jnp.int32)) - 1
    hits = chosen_mask[None, :] & (slot_of[None, :] == jnp.arange(kept, dtype=jnp.int32)[:, None])
    kept_rows = jnp.sum(jnp.where(hits, jnp.arange(block_len, dtype=jnp.int32)[None, :], 0), axis=1)
    fnorm = rms_scale(first_pass, ffn_gain).astype(jnp.bfloat16)
    ffn_rows, down_all = lax.optimization_barrier((fnorm[kept_rows], down_all))
    ffn_kept = run_ffn(ffn_rows, w_gate, w_up, down_all, w_down.shape[0])
    ffn_sum = ffn_kept[jnp.clip(slot_of, 0, kept - 1)]
    placed = first_pass + ffn_sum
    second_in = jnp.where(chosen_mask[:, None], placed, block_rows.astype(jnp.float32))
    refined = attend_block(
        second_in,
        cache_keys,
        cache_vals,
        cache_length,
        attn_gain,
        q_weight,
        k_weight,
        v_weight,
        o_weight,
    )
    return refined[None]


def solution(mesh):
    global BLK, BLK_PARTS
    if dict(mesh.shape) == {"req": 8, "blk": 32}:
        mesh = Mesh(mesh.devices.reshape(8, 4, 4, 2), ("req", "y", "zl", "c"))
        BLK, BLK_PARTS = ("y", "zl", "c"), ("y", "zl", "c")
    rows = ("req",) + (BLK if isinstance(BLK, tuple) else (BLK,))
    return jax.shard_map(
        local,
        mesh=mesh,
        in_specs=(
            P(rows, None, None),
            P(rows, None, None, None),
            P(rows),
            P(rows),
            P(rows, None),
            P(),
            P(),
            P(),
            P(),
            P(),
            P(),
            P(None, BLK),
            P(None, BLK),
            P(BLK, None),
        ),
        out_specs=P(rows, None, None),
        check_vma=False,
    )
```

```python
import jax
import jax.numpy as jnp
from jax import lax
from jax.sharding import PartitionSpec as P

HEAD = 96


norm_eps = 1e-05
rope_base = 100000.0


def rms_scale(values, gain_row):
    return (
        values * lax.rsqrt(jnp.mean(values * values, axis=-1, keepdims=True) + norm_eps) * gain_row
    )


def rotate_heads(flat, positions, head_count):
    half_dim = HEAD // 2
    shaped = flat.reshape(flat.shape[0], head_count, HEAD)
    freqs = jnp.exp(-jnp.log(rope_base) * 2.0 * jnp.arange(half_dim, dtype=jnp.float32) / HEAD)
    angles = positions[:, None] * freqs[None, :]
    cosine = jnp.cos(angles)[:, None, :]
    sine = jnp.sin(angles)[:, None, :]
    first_half = shaped[..., :half_dim]
    second_half = shaped[..., half_dim:]
    turned = jnp.concatenate(
        [first_half * cosine - second_half * sine, second_half * cosine + first_half * sine],
        axis=-1,
    )
    return turned.reshape(flat.shape[0], head_count * HEAD)


def attend_block(
    tok_rows,
    cache_keys,
    cache_vals,
    cache_length,
    attn_gain,
    q_weight,
    k_weight,
    v_weight,
    o_weight,
):
    block_len = tok_rows.shape[0]
    slot_len = cache_keys.shape[0]
    kv_count = k_weight.shape[1] // HEAD
    q_count = q_weight.shape[1] // HEAD
    widened = tok_rows.astype(jnp.float32)
    normed = rms_scale(widened, attn_gain).astype(jnp.bfloat16)
    positions = (cache_length + jnp.arange(block_len, dtype=jnp.int32)).astype(jnp.float32)
    queries = rotate_heads(
        jnp.dot(normed, q_weight, preferred_element_type=jnp.float32), positions, q_count
    ).astype(jnp.bfloat16)
    new_keys = rotate_heads(
        jnp.dot(normed, k_weight, preferred_element_type=jnp.float32), positions, kv_count
    ).astype(jnp.bfloat16)
    new_vals = jnp.dot(normed, v_weight, preferred_element_type=jnp.float32).astype(jnp.bfloat16)
    all_keys = jnp.concatenate([cache_keys, new_keys], axis=0).reshape(
        slot_len + block_len, kv_count, HEAD
    )
    all_vals = jnp.concatenate([cache_vals, new_vals], axis=0).reshape(
        slot_len + block_len, kv_count, HEAD
    )
    grouped = queries.reshape(block_len, kv_count, q_count // kv_count, HEAD)
    scores = jnp.einsum(
        "bgid,kgd->gibk", grouped, all_keys, preferred_element_type=jnp.float32
    ) * HEAD ** (-0.5)
    valid = jnp.concatenate(
        [
            jnp.arange(slot_len, dtype=jnp.int32) < cache_length,
            jnp.ones((block_len,), dtype=jnp.bool_),
        ]
    )
    scores = jnp.where(valid, scores, -jnp.inf)
    peaks = jnp.max(scores, axis=-1, keepdims=True)
    expd = jnp.exp(scores - peaks)
    probs = (expd / jnp.sum(expd, axis=-1, keepdims=True)).astype(jnp.bfloat16)
    context = jnp.einsum("gibk,kgd->bgid", probs, all_vals, preferred_element_type=jnp.float32)
    context = context.astype(jnp.bfloat16).reshape(block_len, q_count * HEAD)
    return widened + jnp.dot(context, o_weight, preferred_element_type=jnp.float32)


def run_ffn(normed_rows, w_gate, w_up, w_down):
    packed = lax.all_gather(jnp.concatenate([normed_rows, w_down], axis=0), "blk", axis=0, tiled=False)
    part_rows = packed[:, : normed_rows.shape[0]].reshape(-1, normed_rows.shape[1])
    down_all = packed[:, normed_rows.shape[0] :].reshape(-1, w_down.shape[1])
    groups = w_down.shape[0]
    gate_vals = jnp.dot(part_rows, w_gate, preferred_element_type=jnp.float32)
    up_vals = jnp.dot(part_rows, w_up, preferred_element_type=jnp.float32)
    hidden_all = (jax.nn.silu(gate_vals) * up_vals).astype(jnp.bfloat16)
    hidden_own = lax.all_to_all(hidden_all, "blk", 0, 1, tiled=True)
    group_count = down_all.shape[0] // groups
    terms = jnp.einsum(
        "rgk,gkd->grd",
        hidden_own.reshape(hidden_own.shape[0], group_count, groups),
        down_all.reshape(group_count, groups, down_all.shape[1]),
        preferred_element_type=jnp.float32,
    ).astype(jnp.bfloat16)
    return jnp.sum(terms.astype(jnp.float32), axis=0)


def fetch_slot(cache_kv, holder):
    count = lax.axis_size("req")
    own = cache_kv[0]
    if count != 8:
        slots = lax.all_gather(own, "req", axis=0, tiled=False)
        return slots[holder[0]]
    me = lax.axis_index("req")

    def swap(values, mask):
        return lax.ppermute(values, "req", perm=[(i, i ^ mask) for i in range(count)])

    def pick(cond, a, b):
        return jnp.where(cond, a, b)

    near = swap(holder, 1)
    quad = swap(jnp.concatenate([holder, near]), 2)
    holders = {0: holder[0], 1: near[0], 2: quad[0], 3: quad[1]}

    got1 = swap(own, 4)
    send_a = pick(holders[2] == (me ^ 4), got1, own)
    send_b = pick(holders[3] == (me ^ 4), got1, own)
    got2 = swap(jnp.stack([send_a, send_b]), 2)
    want = holders[1]
    send_c = pick(want == me, own, pick(want == (me ^ 4), got1, got2[1]))
    got3 = swap(send_c, 1)
    need = holders[0]
    return pick(
        need == me,
        own,
        pick(need == (me ^ 4), got1, pick((need ^ me) == 2, got2[0], pick((need ^ me) == 6, got2[0], got3))),
    )


def local(
    tokens,
    cache_kv,
    cache_len,
    holder,
    accept,
    attn_gain,
    q_weight,
    k_weight,
    v_weight,
    o_weight,
    ffn_gain,
    w_gate,
    w_up,
    w_down,
):
    fetched = fetch_slot(cache_kv, holder)
    cache_keys = fetched[0]
    cache_vals = fetched[1]
    cache_length = cache_len[0]
    block_rows = tokens[0]
    first_pass = attend_block(
        block_rows,
        cache_keys,
        cache_vals,
        cache_length,
        attn_gain,
        q_weight,
        k_weight,
        v_weight,
        o_weight,
    )
    chosen_mask = accept[0] == 1
    block_len = block_rows.shape[0]
    kept = block_len // 2
    slot_of = jnp.cumsum(chosen_mask.astype(jnp.int32)) - 1
    hits = chosen_mask[None, :] & (slot_of[None, :] == jnp.arange(kept, dtype=jnp.int32)[:, None])
    kept_rows = jnp.sum(jnp.where(hits, jnp.arange(block_len, dtype=jnp.int32)[None, :], 0), axis=1)
    fnorm = rms_scale(first_pass, ffn_gain).astype(jnp.bfloat16)
    ffn_kept = run_ffn(fnorm[kept_rows], w_gate, w_up, w_down)
    ffn_sum = ffn_kept[jnp.clip(slot_of, 0, kept - 1)]
    placed = first_pass + ffn_sum
    second_in = jnp.where(chosen_mask[:, None], placed, block_rows.astype(jnp.float32))
    refined = attend_block(
        second_in,
        cache_keys,
        cache_vals,
        cache_length,
        attn_gain,
        q_weight,
        k_weight,
        v_weight,
        o_weight,
    )
    return refined[None]


def solution(mesh):
    return jax.shard_map(
        local,
        mesh=mesh,
        in_specs=(
            P(("req", "blk"), None, None),
            P(("req", "blk"), None, None, None),
            P(("req", "blk")),
            P(("req", "blk")),
            P(("req", "blk"), None),
            P(),
            P(),
            P(),
            P(),
            P(),
            P(),
            P(None, "blk"),
            P(None, "blk"),
            P("blk", None),
        ),
        out_specs=P(("req", "blk"), None, None),
        check_vma=False,
    )
```

```python
import jax
import jax.numpy as jnp
from jax import lax
from jax.sharding import PartitionSpec as P

HEAD = 96


norm_eps = 1e-05
rope_base = 100000.0


def rms_scale(values, gain_row):
    return (
        values * lax.rsqrt(jnp.mean(values * values, axis=-1, keepdims=True) + norm_eps) * gain_row
    )


def rotate_heads(flat, positions, head_count):
    half_dim = HEAD // 2
    shaped = flat.reshape(flat.shape[0], head_count, HEAD)
    freqs = jnp.exp(-jnp.log(rope_base) * 2.0 * jnp.arange(half_dim, dtype=jnp.float32) / HEAD)
    angles = positions[:, None] * freqs[None, :]
    cosine = jnp.cos(angles)[:, None, :]
    sine = jnp.sin(angles)[:, None, :]
    first_half = shaped[..., :half_dim]
    second_half = shaped[..., half_dim:]
    turned = jnp.concatenate(
        [first_half * cosine - second_half * sine, second_half * cosine + first_half * sine],
        axis=-1,
    )
    return turned.reshape(flat.shape[0], head_count * HEAD)


def attend_block(
    tok_rows,
    cache_keys,
    cache_vals,
    cache_length,
    attn_gain,
    q_weight,
    k_weight,
    v_weight,
    o_weight,
):
    block_len = tok_rows.shape[0]
    slot_len = cache_keys.shape[0]
    kv_count = k_weight.shape[1] // HEAD
    q_count = q_weight.shape[1] // HEAD
    widened = tok_rows.astype(jnp.float32)
    normed = rms_scale(widened, attn_gain).astype(jnp.bfloat16)
    positions = (cache_length + jnp.arange(block_len, dtype=jnp.int32)).astype(jnp.float32)
    queries = rotate_heads(
        jnp.dot(normed, q_weight, preferred_element_type=jnp.float32), positions, q_count
    ).astype(jnp.bfloat16)
    new_keys = rotate_heads(
        jnp.dot(normed, k_weight, preferred_element_type=jnp.float32), positions, kv_count
    ).astype(jnp.bfloat16)
    new_vals = jnp.dot(normed, v_weight, preferred_element_type=jnp.float32).astype(jnp.bfloat16)
    all_keys = jnp.concatenate([cache_keys, new_keys], axis=0).reshape(
        slot_len + block_len, kv_count, HEAD
    )
    all_vals = jnp.concatenate([cache_vals, new_vals], axis=0).reshape(
        slot_len + block_len, kv_count, HEAD
    )
    grouped = queries.reshape(block_len, kv_count, q_count // kv_count, HEAD)
    scores = jnp.einsum(
        "bgid,kgd->gibk", grouped, all_keys, preferred_element_type=jnp.float32
    ) * HEAD ** (-0.5)
    valid = jnp.concatenate(
        [
            jnp.arange(slot_len, dtype=jnp.int32) < cache_length,
            jnp.ones((block_len,), dtype=jnp.bool_),
        ]
    )
    scores = jnp.where(valid, scores, -jnp.inf)
    peaks = jnp.max(scores, axis=-1, keepdims=True)
    expd = jnp.exp(scores - peaks)
    probs = (expd / jnp.sum(expd, axis=-1, keepdims=True)).astype(jnp.bfloat16)
    context = jnp.einsum("gibk,kgd->bgid", probs, all_vals, preferred_element_type=jnp.float32)
    context = context.astype(jnp.bfloat16).reshape(block_len, q_count * HEAD)
    return widened + jnp.dot(context, o_weight, preferred_element_type=jnp.float32)


def run_ffn(normed_rows, w_gate, w_up, down_all, groups):
    part_rows = lax.all_gather(normed_rows, "blk", axis=0, tiled=True)
    both = jnp.dot(part_rows, jnp.concatenate([w_gate, w_up], axis=1), preferred_element_type=jnp.float32)
    gate_vals, up_vals = both[:, : w_gate.shape[1]], both[:, w_gate.shape[1] :]
    hidden_all = (jax.nn.silu(gate_vals) * up_vals).astype(jnp.bfloat16)
    hidden_own = lax.all_to_all(hidden_all, "blk", 0, 1, tiled=True)
    group_count = down_all.shape[0] // groups
    terms = jnp.einsum(
        "rgk,gkd->grd",
        hidden_own.reshape(hidden_own.shape[0], group_count, groups),
        down_all.reshape(group_count, groups, down_all.shape[1]),
        preferred_element_type=jnp.float32,
    ).astype(jnp.bfloat16)
    return jnp.sum(terms.astype(jnp.float32), axis=0)


def fetch_slot(cache_kv, holder):
    count = lax.axis_size("req")
    own = cache_kv[0]
    if count != 8:
        slots = lax.all_gather(own, "req", axis=0, tiled=False)
        return slots[holder[0]]
    me = lax.axis_index("req")

    def swap(values, mask):
        return lax.ppermute(values, "req", perm=[(i, i ^ mask) for i in range(count)])

    def pick(cond, a, b):
        return jnp.where(cond, a, b)

    near = swap(holder, 1)
    quad = swap(jnp.concatenate([holder, near]), 2)
    holders = {0: holder[0], 1: near[0], 2: quad[0], 3: quad[1]}

    got1 = swap(own, 4)
    send_a = pick(holders[2] == (me ^ 4), got1, own)
    send_b = pick(holders[3] == (me ^ 4), got1, own)
    got2 = swap(jnp.stack([send_a, send_b]), 2)
    want = holders[1]
    send_c = pick(want == me, own, pick(want == (me ^ 4), got1, got2[1]))
    got3 = swap(send_c, 1)
    need = holders[0]
    return pick(
        need == me,
        own,
        pick(need == (me ^ 4), got1, pick((need ^ me) == 2, got2[0], pick((need ^ me) == 6, got2[0], got3))),
    )


def local(
    tokens,
    cache_kv,
    cache_len,
    holder,
    accept,
    attn_gain,
    q_weight,
    k_weight,
    v_weight,
    o_weight,
    ffn_gain,
    w_gate,
    w_up,
    w_down,
):
    fetched = fetch_slot(cache_kv, holder)
    down_all = lax.all_gather(w_down, "blk", axis=0, tiled=True)
    cache_keys = fetched[0]
    cache_vals = fetched[1]
    cache_length = cache_len[0]
    block_rows = tokens[0]
    first_pass = attend_block(
        block_rows,
        cache_keys,
        cache_vals,
        cache_length,
        attn_gain,
        q_weight,
        k_weight,
        v_weight,
        o_weight,
    )
    chosen_mask = accept[0] == 1
    block_len = block_rows.shape[0]
    kept = block_len // 2
    slot_of = jnp.cumsum(chosen_mask.astype(jnp.int32)) - 1
    hits = chosen_mask[None, :] & (slot_of[None, :] == jnp.arange(kept, dtype=jnp.int32)[:, None])
    kept_rows = jnp.sum(jnp.where(hits, jnp.arange(block_len, dtype=jnp.int32)[None, :], 0), axis=1)
    fnorm = rms_scale(first_pass, ffn_gain).astype(jnp.bfloat16)
    ffn_rows, down_all = lax.optimization_barrier((fnorm[kept_rows], down_all))
    ffn_kept = run_ffn(ffn_rows, w_gate, w_up, down_all, w_down.shape[0])
    ffn_sum = ffn_kept[jnp.clip(slot_of, 0, kept - 1)]
    placed = first_pass + ffn_sum
    second_in = jnp.where(chosen_mask[:, None], placed, block_rows.astype(jnp.float32))
    refined = attend_block(
        second_in,
        cache_keys,
        cache_vals,
        cache_length,
        attn_gain,
        q_weight,
        k_weight,
        v_weight,
        o_weight,
    )
    return refined[None]


def solution(mesh):
    return jax.shard_map(
        local,
        mesh=mesh,
        in_specs=(
            P(("req", "blk"), None, None),
            P(("req", "blk"), None, None, None),
            P(("req", "blk")),
            P(("req", "blk")),
            P(("req", "blk"), None),
            P(),
            P(),
            P(),
            P(),
            P(),
            P(),
            P(None, "blk"),
            P(None, "blk"),
            P("blk", None),
        ),
        out_specs=P(("req", "blk"), None, None),
        check_vma=False,
    )
```

```python
import jax
import jax.numpy as jnp
from jax import lax
from jax.sharding import PartitionSpec as P

HEAD = 96


norm_eps = 1e-05
rope_base = 100000.0


def rms_scale(values, gain_row):
    return (
        values * lax.rsqrt(jnp.mean(values * values, axis=-1, keepdims=True) + norm_eps) * gain_row
    )


def rotate_heads(flat, positions, head_count):
    half_dim = HEAD // 2
    shaped = flat.reshape(flat.shape[0], head_count, HEAD)
    freqs = jnp.exp(-jnp.log(rope_base) * 2.0 * jnp.arange(half_dim, dtype=jnp.float32) / HEAD)
    angles = positions[:, None] * freqs[None, :]
    cosine = jnp.cos(angles)[:, None, :]
    sine = jnp.sin(angles)[:, None, :]
    first_half = shaped[..., :half_dim]
    second_half = shaped[..., half_dim:]
    turned = jnp.concatenate(
        [first_half * cosine - second_half * sine, second_half * cosine + first_half * sine],
        axis=-1,
    )
    return turned.reshape(flat.shape[0], head_count * HEAD)


def attend_block(
    tok_rows,
    cache_keys,
    cache_vals,
    cache_length,
    attn_gain,
    q_weight,
    k_weight,
    v_weight,
    o_weight,
):
    block_len = tok_rows.shape[0]
    slot_len = cache_keys.shape[0]
    kv_count = k_weight.shape[1] // HEAD
    q_count = q_weight.shape[1] // HEAD
    widened = tok_rows.astype(jnp.float32)
    normed = rms_scale(widened, attn_gain).astype(jnp.bfloat16)
    positions = (cache_length + jnp.arange(block_len, dtype=jnp.int32)).astype(jnp.float32)
    queries = rotate_heads(
        jnp.dot(normed, q_weight, preferred_element_type=jnp.float32), positions, q_count
    ).astype(jnp.bfloat16)
    new_keys = rotate_heads(
        jnp.dot(normed, k_weight, preferred_element_type=jnp.float32), positions, kv_count
    ).astype(jnp.bfloat16)
    new_vals = jnp.dot(normed, v_weight, preferred_element_type=jnp.float32).astype(jnp.bfloat16)
    all_keys = jnp.concatenate([cache_keys, new_keys], axis=0).reshape(
        slot_len + block_len, kv_count, HEAD
    )
    all_vals = jnp.concatenate([cache_vals, new_vals], axis=0).reshape(
        slot_len + block_len, kv_count, HEAD
    )
    grouped = queries.reshape(block_len, kv_count, q_count // kv_count, HEAD)
    scores = jnp.einsum(
        "bgid,kgd->gibk", grouped, all_keys, preferred_element_type=jnp.float32
    ) * HEAD ** (-0.5)
    valid = jnp.concatenate(
        [
            jnp.arange(slot_len, dtype=jnp.int32) < cache_length,
            jnp.ones((block_len,), dtype=jnp.bool_),
        ]
    )
    scores = jnp.where(valid, scores, -jnp.inf)
    peaks = jnp.max(scores, axis=-1, keepdims=True)
    expd = jnp.exp(scores - peaks)
    probs = (expd / jnp.sum(expd, axis=-1, keepdims=True)).astype(jnp.bfloat16)
    context = jnp.einsum("gibk,kgd->bgid", probs, all_vals, preferred_element_type=jnp.float32)
    context = context.astype(jnp.bfloat16).reshape(block_len, q_count * HEAD)
    return widened + jnp.dot(context, o_weight, preferred_element_type=jnp.float32)


def run_ffn(normed_rows, w_gate, w_up, down_all, groups):
    part_rows = lax.all_gather(normed_rows, "blk", axis=0, tiled=True)
    both = jnp.dot(part_rows, jnp.concatenate([w_gate, w_up], axis=1), preferred_element_type=jnp.float32)
    gate_vals, up_vals = both[:, : w_gate.shape[1]], both[:, w_gate.shape[1] :]
    hidden_all = (jax.nn.silu(gate_vals) * up_vals).astype(jnp.bfloat16)
    hidden_own = lax.all_to_all(hidden_all, "blk", 0, 1, tiled=True)
    group_count = down_all.shape[0] // groups
    terms = jnp.einsum(
        "rgk,gkd->grd",
        hidden_own.reshape(hidden_own.shape[0], group_count, groups),
        down_all.reshape(group_count, groups, down_all.shape[1]),
        preferred_element_type=jnp.float32,
    ).astype(jnp.bfloat16)
    return jnp.sum(terms.astype(jnp.float32), axis=0)


def fetch_slot(cache_kv, holder):
    count = lax.axis_size("req")
    own = cache_kv[0]
    if count != 8:
        slots = lax.all_gather(own, "req", axis=0, tiled=False)
        return slots[holder[0]], own
    me = lax.axis_index("req")

    def swap(values, mask):
        return lax.ppermute(values, "req", perm=[(i, i ^ mask) for i in range(count)])

    def pick(cond, a, b):
        return jnp.where(cond, a, b)

    far = swap(holder, 4)
    pair = swap(jnp.concatenate([holder, far]), 2)
    holders = {0: holder[0], 4: far[0], 2: pair[0], 6: pair[1]}

    got1 = swap(own, 1)
    send_a = pick(holders[2] == (me ^ 1), got1, own)
    send_b = pick(holders[6] == (me ^ 1), got1, own)
    got2 = swap(jnp.stack([send_a, send_b]), 2)
    want = holders[4]
    send_c = pick(want == me, own, pick(want == (me ^ 1), got1, got2[1]))
    got3 = swap(send_c, 4)
    need = holders[0]
    slot = pick(
        need == me,
        own,
        pick(need == (me ^ 1), got1, pick(((need ^ me) >> 1) == 1, got2[0], got3)),
    )
    return slot, got1


def local(
    tokens,
    cache_kv,
    cache_len,
    holder,
    accept,
    attn_gain,
    q_weight,
    k_weight,
    v_weight,
    o_weight,
    ffn_gain,
    w_gate,
    w_up,
    w_down,
):
    fetched, _ = fetch_slot(cache_kv, holder)
    down_all = lax.all_gather(w_down, "blk", axis=0, tiled=True)
    cache_keys = fetched[0]
    cache_vals = fetched[1]
    cache_length = cache_len[0]
    block_rows = tokens[0]
    first_pass = attend_block(
        block_rows,
        cache_keys,
        cache_vals,
        cache_length,
        attn_gain,
        q_weight,
        k_weight,
        v_weight,
        o_weight,
    )
    chosen_mask = accept[0] == 1
    block_len = block_rows.shape[0]
    kept = block_len // 2
    slot_of = jnp.cumsum(chosen_mask.astype(jnp.int32)) - 1
    hits = chosen_mask[None, :] & (slot_of[None, :] == jnp.arange(kept, dtype=jnp.int32)[:, None])
    kept_rows = jnp.sum(jnp.where(hits, jnp.arange(block_len, dtype=jnp.int32)[None, :], 0), axis=1)
    fnorm = rms_scale(first_pass, ffn_gain).astype(jnp.bfloat16)
    ffn_rows, down_all = lax.optimization_barrier((fnorm[kept_rows], down_all))
    ffn_kept = run_ffn(ffn_rows, w_gate, w_up, down_all, w_down.shape[0])
    ffn_sum = ffn_kept[jnp.clip(slot_of, 0, kept - 1)]
    placed = first_pass + ffn_sum
    second_in = jnp.where(chosen_mask[:, None], placed, block_rows.astype(jnp.float32))
    refined = attend_block(
        second_in,
        cache_keys,
        cache_vals,
        cache_length,
        attn_gain,
        q_weight,
        k_weight,
        v_weight,
        o_weight,
    )
    return refined[None]


def solution(mesh):
    return jax.shard_map(
        local,
        mesh=mesh,
        in_specs=(
            P(("req", "blk"), None, None),
            P(("req", "blk"), None, None, None),
            P(("req", "blk")),
            P(("req", "blk")),
            P(("req", "blk"), None),
            P(),
            P(),
            P(),
            P(),
            P(),
            P(),
            P(None, "blk"),
            P(None, "blk"),
            P("blk", None),
        ),
        out_specs=P(("req", "blk"), None, None),
        check_vma=False,
    )
```

```python
import jax
import jax.numpy as jnp
from jax import lax
from jax.sharding import PartitionSpec as P

HEAD = 96


norm_eps = 1e-05
rope_base = 100000.0


def rms_scale(values, gain_row):
    return (
        values * lax.rsqrt(jnp.mean(values * values, axis=-1, keepdims=True) + norm_eps) * gain_row
    )


def rotate_heads(flat, positions, head_count):
    half_dim = HEAD // 2
    shaped = flat.reshape(flat.shape[0], head_count, HEAD)
    freqs = jnp.exp(-jnp.log(rope_base) * 2.0 * jnp.arange(half_dim, dtype=jnp.float32) / HEAD)
    angles = positions[:, None] * freqs[None, :]
    cosine = jnp.cos(angles)[:, None, :]
    sine = jnp.sin(angles)[:, None, :]
    first_half = shaped[..., :half_dim]
    second_half = shaped[..., half_dim:]
    turned = jnp.concatenate(
        [first_half * cosine - second_half * sine, second_half * cosine + first_half * sine],
        axis=-1,
    )
    return turned.reshape(flat.shape[0], head_count * HEAD)


def attend_block(
    tok_rows,
    cache_keys,
    cache_vals,
    cache_length,
    attn_gain,
    q_weight,
    k_weight,
    v_weight,
    o_weight,
):
    block_len = tok_rows.shape[0]
    slot_len = cache_keys.shape[0]
    kv_count = k_weight.shape[1] // HEAD
    q_count = q_weight.shape[1] // HEAD
    widened = tok_rows.astype(jnp.float32)
    normed = rms_scale(widened, attn_gain).astype(jnp.bfloat16)
    positions = (cache_length + jnp.arange(block_len, dtype=jnp.int32)).astype(jnp.float32)
    queries = rotate_heads(
        jnp.dot(normed, q_weight, preferred_element_type=jnp.float32), positions, q_count
    ).astype(jnp.bfloat16)
    new_keys = rotate_heads(
        jnp.dot(normed, k_weight, preferred_element_type=jnp.float32), positions, kv_count
    ).astype(jnp.bfloat16)
    new_vals = jnp.dot(normed, v_weight, preferred_element_type=jnp.float32).astype(jnp.bfloat16)
    all_keys = jnp.concatenate([cache_keys, new_keys], axis=0).reshape(
        slot_len + block_len, kv_count, HEAD
    )
    all_vals = jnp.concatenate([cache_vals, new_vals], axis=0).reshape(
        slot_len + block_len, kv_count, HEAD
    )
    grouped = queries.reshape(block_len, kv_count, q_count // kv_count, HEAD)
    scores = jnp.einsum(
        "bgid,kgd->gibk", grouped, all_keys, preferred_element_type=jnp.float32
    ) * HEAD ** (-0.5)
    valid = jnp.concatenate(
        [
            jnp.arange(slot_len, dtype=jnp.int32) < cache_length,
            jnp.ones((block_len,), dtype=jnp.bool_),
        ]
    )
    scores = jnp.where(valid, scores, -jnp.inf)
    peaks = jnp.max(scores, axis=-1, keepdims=True)
    expd = jnp.exp(scores - peaks)
    probs = (expd / jnp.sum(expd, axis=-1, keepdims=True)).astype(jnp.bfloat16)
    context = jnp.einsum("gibk,kgd->bgid", probs, all_vals, preferred_element_type=jnp.float32)
    context = context.astype(jnp.bfloat16).reshape(block_len, q_count * HEAD)
    return widened + jnp.dot(context, o_weight, preferred_element_type=jnp.float32)


def run_ffn(normed_rows, w_gate, w_up, down_all, groups):
    part_rows = lax.all_gather(normed_rows, "blk", axis=0, tiled=True)
    both = jnp.dot(part_rows, jnp.concatenate([w_gate, w_up], axis=1), preferred_element_type=jnp.float32)
    gate_vals, up_vals = both[:, : w_gate.shape[1]], both[:, w_gate.shape[1] :]
    hidden_all = (jax.nn.silu(gate_vals) * up_vals).astype(jnp.bfloat16)
    hidden_own = lax.all_to_all(hidden_all, "blk", 0, 1, tiled=True)
    return jnp.dot(hidden_own, down_all, preferred_element_type=jnp.float32)


def fetch_slot(cache_kv, holder):
    count = lax.axis_size("req")
    own = cache_kv[0]
    if count != 8:
        slots = lax.all_gather(own, "req", axis=0, tiled=False)
        return slots[holder[0]], own
    me = lax.axis_index("req")

    def swap(values, mask):
        return lax.ppermute(values, "req", perm=[(i, i ^ mask) for i in range(count)])

    def pick(cond, a, b):
        return jnp.where(cond, a, b)

    far = swap(holder, 4)
    pair = swap(jnp.concatenate([holder, far]), 2)
    holders = {0: holder[0], 4: far[0], 2: pair[0], 6: pair[1]}

    got1 = swap(own, 1)
    send_a = pick(holders[2] == (me ^ 1), got1, own)
    send_b = pick(holders[6] == (me ^ 1), got1, own)
    got2 = swap(jnp.stack([send_a, send_b]), 2)
    want = holders[4]
    send_c = pick(want == me, own, pick(want == (me ^ 1), got1, got2[1]))
    got3 = swap(send_c, 4)
    need = holders[0]
    slot = pick(
        need == me,
        own,
        pick(need == (me ^ 1), got1, pick(((need ^ me) >> 1) == 1, got2[0], got3)),
    )
    return slot, got1


def local(
    tokens,
    cache_kv,
    cache_len,
    holder,
    accept,
    attn_gain,
    q_weight,
    k_weight,
    v_weight,
    o_weight,
    ffn_gain,
    w_gate,
    w_up,
    w_down,
):
    fetched, _ = fetch_slot(cache_kv, holder)
    down_all = lax.all_gather(w_down, "blk", axis=0, tiled=True)
    cache_keys = fetched[0]
    cache_vals = fetched[1]
    cache_length = cache_len[0]
    block_rows = tokens[0]
    first_pass = attend_block(
        block_rows,
        cache_keys,
        cache_vals,
        cache_length,
        attn_gain,
        q_weight,
        k_weight,
        v_weight,
        o_weight,
    )
    chosen_mask = accept[0] == 1
    block_len = block_rows.shape[0]
    kept = block_len // 2
    slot_of = jnp.cumsum(chosen_mask.astype(jnp.int32)) - 1
    hits = chosen_mask[None, :] & (slot_of[None, :] == jnp.arange(kept, dtype=jnp.int32)[:, None])
    kept_rows = jnp.sum(jnp.where(hits, jnp.arange(block_len, dtype=jnp.int32)[None, :], 0), axis=1)
    fnorm = rms_scale(first_pass, ffn_gain).astype(jnp.bfloat16)
    ffn_rows, down_all = lax.optimization_barrier((fnorm[kept_rows], down_all))
    ffn_kept = run_ffn(ffn_rows, w_gate, w_up, down_all, w_down.shape[0])
    ffn_sum = ffn_kept[jnp.clip(slot_of, 0, kept - 1)]
    placed = first_pass + ffn_sum
    second_in = jnp.where(chosen_mask[:, None], placed, block_rows.astype(jnp.float32))
    refined = attend_block(
        second_in,
        cache_keys,
        cache_vals,
        cache_length,
        attn_gain,
        q_weight,
        k_weight,
        v_weight,
        o_weight,
    )
    return refined[None]


def solution(mesh):
    return jax.shard_map(
        local,
        mesh=mesh,
        in_specs=(
            P(("req", "blk"), None, None),
            P(("req", "blk"), None, None, None),
            P(("req", "blk")),
            P(("req", "blk")),
            P(("req", "blk"), None),
            P(),
            P(),
            P(),
            P(),
            P(),
            P(),
            P(None, "blk"),
            P(None, "blk"),
            P("blk", None),
        ),
        out_specs=P(("req", "blk"), None, None),
        check_vma=False,
    )
```

```python
import jax
import jax.numpy as jnp
from jax import lax
from jax.sharding import PartitionSpec as P

HEAD = 96


norm_eps = 1e-05
rope_base = 100000.0


def rms_scale(values, gain_row):
    return (
        values * lax.rsqrt(jnp.mean(values * values, axis=-1, keepdims=True) + norm_eps) * gain_row
    )


def rotate_heads(flat, positions, head_count):
    half_dim = HEAD // 2
    shaped = flat.reshape(flat.shape[0], head_count, HEAD)
    freqs = jnp.exp(-jnp.log(rope_base) * 2.0 * jnp.arange(half_dim, dtype=jnp.float32) / HEAD)
    angles = positions[:, None] * freqs[None, :]
    cosine = jnp.cos(angles)[:, None, :]
    sine = jnp.sin(angles)[:, None, :]
    first_half = shaped[..., :half_dim]
    second_half = shaped[..., half_dim:]
    turned = jnp.concatenate(
        [first_half * cosine - second_half * sine, second_half * cosine + first_half * sine],
        axis=-1,
    )
    return turned.reshape(flat.shape[0], head_count * HEAD)


def attend_block(
    tok_rows,
    cache_keys,
    cache_vals,
    cache_length,
    attn_gain,
    q_weight,
    k_weight,
    v_weight,
    o_weight,
):
    block_len = tok_rows.shape[0]
    slot_len = cache_keys.shape[0]
    kv_count = k_weight.shape[1] // HEAD
    q_count = q_weight.shape[1] // HEAD
    widened = tok_rows.astype(jnp.float32)
    normed = rms_scale(widened, attn_gain).astype(jnp.bfloat16)
    positions = (cache_length + jnp.arange(block_len, dtype=jnp.int32)).astype(jnp.float32)
    queries = rotate_heads(
        jnp.dot(normed, q_weight, preferred_element_type=jnp.float32), positions, q_count
    ).astype(jnp.bfloat16)
    new_keys = rotate_heads(
        jnp.dot(normed, k_weight, preferred_element_type=jnp.float32), positions, kv_count
    ).astype(jnp.bfloat16)
    new_vals = jnp.dot(normed, v_weight, preferred_element_type=jnp.float32).astype(jnp.bfloat16)
    all_keys = jnp.concatenate([cache_keys, new_keys], axis=0).reshape(
        slot_len + block_len, kv_count, HEAD
    )
    all_vals = jnp.concatenate([cache_vals, new_vals], axis=0).reshape(
        slot_len + block_len, kv_count, HEAD
    )
    grouped = queries.reshape(block_len, kv_count, q_count // kv_count, HEAD)
    scores = jnp.einsum(
        "bgid,kgd->gibk", grouped, all_keys, preferred_element_type=jnp.float32
    ) * HEAD ** (-0.5)
    valid = jnp.concatenate(
        [
            jnp.arange(slot_len, dtype=jnp.int32) < cache_length,
            jnp.ones((block_len,), dtype=jnp.bool_),
        ]
    )
    scores = jnp.where(valid, scores, -jnp.inf)
    peaks = jnp.max(scores, axis=-1, keepdims=True)
    expd = jnp.exp(scores - peaks)
    probs = (expd / jnp.sum(expd, axis=-1, keepdims=True)).astype(jnp.bfloat16)
    context = jnp.einsum("gibk,kgd->bgid", probs, all_vals, preferred_element_type=jnp.float32)
    context = context.astype(jnp.bfloat16).reshape(block_len, q_count * HEAD)
    return widened + jnp.dot(context, o_weight, preferred_element_type=jnp.float32)


def run_ffn(normed_rows, w_gate, w_up, down_all, groups):
    part_rows = lax.all_gather(normed_rows, "blk", axis=0, tiled=True)
    both = jnp.dot(part_rows, jnp.concatenate([w_gate, w_up], axis=1), preferred_element_type=jnp.float32)
    gate_vals, up_vals = both[:, : w_gate.shape[1]], both[:, w_gate.shape[1] :]
    hidden_all = (jax.nn.silu(gate_vals) * up_vals).astype(jnp.bfloat16)
    hidden_own = lax.all_to_all(hidden_all, "blk", 0, 1, tiled=True)
    group_count = down_all.shape[0] // groups
    terms = jnp.einsum(
        "rgk,gkd->grd",
        hidden_own.reshape(hidden_own.shape[0], group_count, groups),
        down_all.reshape(group_count, groups, down_all.shape[1]),
        preferred_element_type=jnp.float32,
    ).astype(jnp.bfloat16)
    return jnp.sum(terms.astype(jnp.float32), axis=0)


def fetch_slot(cache_kv, holder, anchor):
    count = lax.axis_size("req")
    own = cache_kv[0]
    if count != 8:
        slots = lax.all_gather(own, "req", axis=0, tiled=False)
        return slots[holder[0]], own
    me = lax.axis_index("req")

    def swap(values, mask):
        return lax.ppermute(values, "req", perm=[(i, i ^ mask) for i in range(count)])

    def pick(cond, a, b):
        return jnp.where(cond, a, b)

    far = swap(holder, 4)
    pair = swap(jnp.concatenate([holder, far]), 2)
    holders = {0: holder[0], 4: far[0], 2: pair[0], 6: pair[1]}

    got1 = swap(own, 1)
    got1, _ = lax.optimization_barrier((got1, anchor))
    send_a = pick(holders[2] == (me ^ 1), got1, own)
    send_b = pick(holders[6] == (me ^ 1), got1, own)
    got2 = swap(jnp.stack([send_a, send_b]), 2)
    want = holders[4]
    send_c = pick(want == me, own, pick(want == (me ^ 1), got1, got2[1]))
    got3 = swap(send_c, 4)
    need = holders[0]
    slot = pick(
        need == me,
        own,
        pick(need == (me ^ 1), got1, pick(((need ^ me) >> 1) == 1, got2[0], got3)),
    )
    return slot, got1


def local(
    tokens,
    cache_kv,
    cache_len,
    holder,
    accept,
    attn_gain,
    q_weight,
    k_weight,
    v_weight,
    o_weight,
    ffn_gain,
    w_gate,
    w_up,
    w_down,
):
    anchor = jnp.dot(
        rms_scale(tokens[0].astype(jnp.float32), attn_gain).astype(jnp.bfloat16),
        q_weight,
        preferred_element_type=jnp.float32,
    )
    fetched, _ = fetch_slot(cache_kv, holder, anchor)
    down_all = lax.all_gather(w_down, "blk", axis=0, tiled=True)
    cache_keys = fetched[0]
    cache_vals = fetched[1]
    cache_length = cache_len[0]
    block_rows = tokens[0]
    first_pass = attend_block(
        block_rows,
        cache_keys,
        cache_vals,
        cache_length,
        attn_gain,
        q_weight,
        k_weight,
        v_weight,
        o_weight,
    )
    chosen_mask = accept[0] == 1
    block_len = block_rows.shape[0]
    kept = block_len // 2
    slot_of = jnp.cumsum(chosen_mask.astype(jnp.int32)) - 1
    hits = chosen_mask[None, :] & (slot_of[None, :] == jnp.arange(kept, dtype=jnp.int32)[:, None])
    kept_rows = jnp.sum(jnp.where(hits, jnp.arange(block_len, dtype=jnp.int32)[None, :], 0), axis=1)
    fnorm = rms_scale(first_pass, ffn_gain).astype(jnp.bfloat16)
    ffn_rows, down_all = lax.optimization_barrier((fnorm[kept_rows], down_all))
    ffn_kept = run_ffn(ffn_rows, w_gate, w_up, down_all, w_down.shape[0])
    ffn_sum = ffn_kept[jnp.clip(slot_of, 0, kept - 1)]
    placed = first_pass + ffn_sum
    second_in = jnp.where(chosen_mask[:, None], placed, block_rows.astype(jnp.float32))
    refined = attend_block(
        second_in,
        cache_keys,
        cache_vals,
        cache_length,
        attn_gain,
        q_weight,
        k_weight,
        v_weight,
        o_weight,
    )
    return refined[None]


def solution(mesh):
    return jax.shard_map(
        local,
        mesh=mesh,
        in_specs=(
            P(("req", "blk"), None, None),
            P(("req", "blk"), None, None, None),
            P(("req", "blk")),
            P(("req", "blk")),
            P(("req", "blk"), None),
            P(),
            P(),
            P(),
            P(),
            P(),
            P(),
            P(None, "blk"),
            P(None, "blk"),
            P("blk", None),
        ),
        out_specs=P(("req", "blk"), None, None),
        check_vma=False,
    )
```

```python
import jax
import jax.numpy as jnp
from jax import lax
from jax.sharding import PartitionSpec as P

HEAD = 96


norm_eps = 1e-05
rope_base = 100000.0


def rms_scale(values, gain_row):
    return (
        values * lax.rsqrt(jnp.mean(values * values, axis=-1, keepdims=True) + norm_eps) * gain_row
    )


def rotate_heads(flat, positions, head_count):
    half_dim = HEAD // 2
    shaped = flat.reshape(flat.shape[0], head_count, HEAD)
    freqs = jnp.exp(-jnp.log(rope_base) * 2.0 * jnp.arange(half_dim, dtype=jnp.float32) / HEAD)
    angles = positions[:, None] * freqs[None, :]
    cosine = jnp.cos(angles)[:, None, :]
    sine = jnp.sin(angles)[:, None, :]
    first_half = shaped[..., :half_dim]
    second_half = shaped[..., half_dim:]
    turned = jnp.concatenate(
        [first_half * cosine - second_half * sine, second_half * cosine + first_half * sine],
        axis=-1,
    )
    return turned.reshape(flat.shape[0], head_count * HEAD)


def attend_block(
    tok_rows,
    cache_keys,
    cache_vals,
    cache_length,
    attn_gain,
    q_weight,
    k_weight,
    v_weight,
    o_weight,
):
    block_len = tok_rows.shape[0]
    slot_len = cache_keys.shape[0]
    kv_count = k_weight.shape[1] // HEAD
    q_count = q_weight.shape[1] // HEAD
    widened = tok_rows.astype(jnp.float32)
    normed = rms_scale(widened, attn_gain).astype(jnp.bfloat16)
    positions = (cache_length + jnp.arange(block_len, dtype=jnp.int32)).astype(jnp.float32)
    queries = rotate_heads(
        jnp.dot(normed, q_weight, preferred_element_type=jnp.float32), positions, q_count
    ).astype(jnp.bfloat16)
    new_keys = rotate_heads(
        jnp.dot(normed, k_weight, preferred_element_type=jnp.float32), positions, kv_count
    ).astype(jnp.bfloat16)
    new_vals = jnp.dot(normed, v_weight, preferred_element_type=jnp.float32).astype(jnp.bfloat16)
    all_keys = jnp.concatenate([cache_keys, new_keys], axis=0).reshape(
        slot_len + block_len, kv_count, HEAD
    )
    all_vals = jnp.concatenate([cache_vals, new_vals], axis=0).reshape(
        slot_len + block_len, kv_count, HEAD
    )
    grouped = queries.reshape(block_len, kv_count, q_count // kv_count, HEAD)
    scores = jnp.einsum(
        "bgid,kgd->gibk", grouped, all_keys, preferred_element_type=jnp.float32
    ) * HEAD ** (-0.5)
    valid = jnp.concatenate(
        [
            jnp.arange(slot_len, dtype=jnp.int32) < cache_length,
            jnp.ones((block_len,), dtype=jnp.bool_),
        ]
    )
    scores = jnp.where(valid, scores, -jnp.inf)
    peaks = jnp.max(scores, axis=-1, keepdims=True)
    expd = jnp.exp(scores - peaks)
    probs = (expd / jnp.sum(expd, axis=-1, keepdims=True)).astype(jnp.bfloat16)
    context = jnp.einsum("gibk,kgd->bgid", probs, all_vals, preferred_element_type=jnp.float32)
    context = context.astype(jnp.bfloat16).reshape(block_len, q_count * HEAD)
    return widened + jnp.dot(context, o_weight, preferred_element_type=jnp.float32)


def run_ffn(normed_rows, w_gate, w_up, down_all, groups, row_slots):
    part_rows = lax.all_gather(normed_rows, "blk", axis=0, tiled=True)
    both = jnp.dot(part_rows, jnp.concatenate([w_gate, w_up], axis=1), preferred_element_type=jnp.float32)
    gate_vals, up_vals = both[:, : w_gate.shape[1]], both[:, w_gate.shape[1] :]
    hidden_all = (jax.nn.silu(gate_vals) * up_vals).astype(jnp.bfloat16)
    hidden_own = lax.all_to_all(hidden_all, "blk", 0, 1, tiled=True)
    hidden_own = hidden_own[row_slots]
    group_count = down_all.shape[0] // groups
    terms = jnp.einsum(
        "rgk,gkd->grd",
        hidden_own.reshape(hidden_own.shape[0], group_count, groups),
        down_all.reshape(group_count, groups, down_all.shape[1]),
        preferred_element_type=jnp.float32,
    ).astype(jnp.bfloat16)
    return jnp.sum(terms.astype(jnp.float32), axis=0)


def fetch_slot(cache_kv, holder, anchor):
    count = lax.axis_size("req")
    own = cache_kv[0]
    if count != 8:
        slots = lax.all_gather(own, "req", axis=0, tiled=False)
        return slots[holder[0]], own
    me = lax.axis_index("req")

    def swap(values, mask):
        return lax.ppermute(values, "req", perm=[(i, i ^ mask) for i in range(count)])

    def pick(cond, a, b):
        return jnp.where(cond, a, b)

    far = swap(holder, 4)
    pair = swap(jnp.concatenate([holder, far]), 2)
    holders = {0: holder[0], 4: far[0], 2: pair[0], 6: pair[1]}

    got1 = swap(own, 1)
    got1, _ = lax.optimization_barrier((got1, anchor))
    send_a = pick(holders[2] == (me ^ 1), got1, own)
    send_b = pick(holders[6] == (me ^ 1), got1, own)
    got2 = swap(jnp.stack([send_a, send_b]), 2)
    want = holders[4]
    send_c = pick(want == me, own, pick(want == (me ^ 1), got1, got2[1]))
    got3 = swap(send_c, 4)
    need = holders[0]
    slot = pick(
        need == me,
        own,
        pick(need == (me ^ 1), got1, pick(((need ^ me) >> 1) == 1, got2[0], got3)),
    )
    return slot, got1


def local(
    tokens,
    cache_kv,
    cache_len,
    holder,
    accept,
    attn_gain,
    q_weight,
    k_weight,
    v_weight,
    o_weight,
    ffn_gain,
    w_gate,
    w_up,
    w_down,
):
    anchor = jnp.dot(
        rms_scale(tokens[0].astype(jnp.float32), attn_gain).astype(jnp.bfloat16),
        q_weight,
        preferred_element_type=jnp.float32,
    )
    fetched, _ = fetch_slot(cache_kv, holder, anchor)
    down_all = lax.all_gather(w_down, "blk", axis=0, tiled=True)
    cache_keys = fetched[0]
    cache_vals = fetched[1]
    cache_length = cache_len[0]
    block_rows = tokens[0]
    first_pass = attend_block(
        block_rows,
        cache_keys,
        cache_vals,
        cache_length,
        attn_gain,
        q_weight,
        k_weight,
        v_weight,
        o_weight,
    )
    chosen_mask = accept[0] == 1
    block_len = block_rows.shape[0]
    kept = block_len // 2
    slot_of = jnp.cumsum(chosen_mask.astype(jnp.int32)) - 1
    hits = chosen_mask[None, :] & (slot_of[None, :] == jnp.arange(kept, dtype=jnp.int32)[:, None])
    kept_rows = jnp.sum(jnp.where(hits, jnp.arange(block_len, dtype=jnp.int32)[None, :], 0), axis=1)
    fnorm = rms_scale(first_pass, ffn_gain).astype(jnp.bfloat16)
    ffn_rows, down_all = lax.optimization_barrier((fnorm[kept_rows], down_all))
    ffn_sum = run_ffn(ffn_rows, w_gate, w_up, down_all, w_down.shape[0], jnp.clip(slot_of, 0, kept - 1))
    placed = first_pass + ffn_sum
    second_in = jnp.where(chosen_mask[:, None], placed, block_rows.astype(jnp.float32))
    refined = attend_block(
        second_in,
        cache_keys,
        cache_vals,
        cache_length,
        attn_gain,
        q_weight,
        k_weight,
        v_weight,
        o_weight,
    )
    return refined[None]


def solution(mesh):
    return jax.shard_map(
        local,
        mesh=mesh,
        in_specs=(
            P(("req", "blk"), None, None),
            P(("req", "blk"), None, None, None),
            P(("req", "blk")),
            P(("req", "blk")),
            P(("req", "blk"), None),
            P(),
            P(),
            P(),
            P(),
            P(),
            P(),
            P(None, "blk"),
            P(None, "blk"),
            P("blk", None),
        ),
        out_specs=P(("req", "blk"), None, None),
        check_vma=False,
    )
```

```python
import jax
import jax.numpy as jnp
from jax import lax
from jax.sharding import PartitionSpec as P

HEAD = 96


norm_eps = 1e-05
rope_base = 100000.0


def rms_scale(values, gain_row):
    return (
        values * lax.rsqrt(jnp.mean(values * values, axis=-1, keepdims=True) + norm_eps) * gain_row
    )


def rotate_heads(flat, positions, head_count):
    half_dim = HEAD // 2
    shaped = flat.reshape(flat.shape[0], head_count, HEAD)
    freqs = jnp.exp(-jnp.log(rope_base) * 2.0 * jnp.arange(half_dim, dtype=jnp.float32) / HEAD)
    angles = positions[:, None] * freqs[None, :]
    cosine = jnp.cos(angles)[:, None, :]
    sine = jnp.sin(angles)[:, None, :]
    first_half = shaped[..., :half_dim]
    second_half = shaped[..., half_dim:]
    turned = jnp.concatenate(
        [first_half * cosine - second_half * sine, second_half * cosine + first_half * sine],
        axis=-1,
    )
    return turned.reshape(flat.shape[0], head_count * HEAD)


def attend_block(
    tok_rows,
    cache_keys,
    cache_vals,
    cache_length,
    attn_gain,
    q_weight,
    k_weight,
    v_weight,
    o_weight,
):
    block_len = tok_rows.shape[0]
    slot_len = cache_keys.shape[0]
    kv_count = k_weight.shape[1] // HEAD
    q_count = q_weight.shape[1] // HEAD
    widened = tok_rows.astype(jnp.float32)
    normed = rms_scale(widened, attn_gain).astype(jnp.bfloat16)
    positions = (cache_length + jnp.arange(block_len, dtype=jnp.int32)).astype(jnp.float32)
    qw, kw = q_weight.shape[1], k_weight.shape[1]
    projected = jnp.dot(
        normed, jnp.concatenate([q_weight, k_weight, v_weight], axis=1), preferred_element_type=jnp.float32
    )
    queries = rotate_heads(projected[:, :qw], positions, q_count).astype(jnp.bfloat16)
    new_keys = rotate_heads(projected[:, qw : qw + kw], positions, kv_count).astype(jnp.bfloat16)
    new_vals = projected[:, qw + kw :].astype(jnp.bfloat16)
    all_keys = jnp.concatenate([cache_keys, new_keys], axis=0).reshape(
        slot_len + block_len, kv_count, HEAD
    )
    all_vals = jnp.concatenate([cache_vals, new_vals], axis=0).reshape(
        slot_len + block_len, kv_count, HEAD
    )
    grouped = queries.reshape(block_len, kv_count, q_count // kv_count, HEAD)
    scores = jnp.einsum(
        "bgid,kgd->gibk", grouped, all_keys, preferred_element_type=jnp.float32
    ) * HEAD ** (-0.5)
    valid = jnp.concatenate(
        [
            jnp.arange(slot_len, dtype=jnp.int32) < cache_length,
            jnp.ones((block_len,), dtype=jnp.bool_),
        ]
    )
    scores = jnp.where(valid, scores, -jnp.inf)
    peaks = jnp.max(scores, axis=-1, keepdims=True)
    expd = jnp.exp(scores - peaks)
    probs = (expd / jnp.sum(expd, axis=-1, keepdims=True)).astype(jnp.bfloat16)
    context = jnp.einsum("gibk,kgd->bgid", probs, all_vals, preferred_element_type=jnp.float32)
    context = context.astype(jnp.bfloat16).reshape(block_len, q_count * HEAD)
    return widened + jnp.dot(context, o_weight, preferred_element_type=jnp.float32)


def run_ffn(normed_rows, w_gate, w_up, down_all, groups):
    part_rows = lax.all_gather(normed_rows, "blk", axis=0, tiled=True)
    both = jnp.dot(part_rows, jnp.concatenate([w_gate, w_up], axis=1), preferred_element_type=jnp.float32)
    gate_vals, up_vals = both[:, : w_gate.shape[1]], both[:, w_gate.shape[1] :]
    hidden_all = (jax.nn.silu(gate_vals) * up_vals).astype(jnp.bfloat16)
    hidden_own = lax.all_to_all(hidden_all, "blk", 0, 1, tiled=True)
    group_count = down_all.shape[0] // groups
    terms = jnp.einsum(
        "rgk,gkd->grd",
        hidden_own.reshape(hidden_own.shape[0], group_count, groups),
        down_all.reshape(group_count, groups, down_all.shape[1]),
        preferred_element_type=jnp.float32,
    ).astype(jnp.bfloat16)
    return jnp.sum(terms.astype(jnp.float32), axis=0)


def fetch_slot(cache_kv, holder, anchor):
    count = lax.axis_size("req")
    own = cache_kv[0]
    if count != 8:
        slots = lax.all_gather(own, "req", axis=0, tiled=False)
        return slots[holder[0]], own
    me = lax.axis_index("req")

    def swap(values, mask):
        return lax.ppermute(values, "req", perm=[(i, i ^ mask) for i in range(count)])

    def pick(cond, a, b):
        return jnp.where(cond, a, b)

    far = swap(holder, 4)
    pair = swap(jnp.concatenate([holder, far]), 2)
    holders = {0: holder[0], 4: far[0], 2: pair[0], 6: pair[1]}

    got1 = swap(own, 1)
    got1, _ = lax.optimization_barrier((got1, anchor))
    send_a = pick(holders[2] == (me ^ 1), got1, own)
    send_b = pick(holders[6] == (me ^ 1), got1, own)
    got2 = swap(jnp.stack([send_a, send_b]), 2)
    want = holders[4]
    send_c = pick(want == me, own, pick(want == (me ^ 1), got1, got2[1]))
    got3 = swap(send_c, 4)
    need = holders[0]
    slot = pick(
        need == me,
        own,
        pick(need == (me ^ 1), got1, pick(((need ^ me) >> 1) == 1, got2[0], got3)),
    )
    return slot, got1


def local(
    tokens,
    cache_kv,
    cache_len,
    holder,
    accept,
    attn_gain,
    q_weight,
    k_weight,
    v_weight,
    o_weight,
    ffn_gain,
    w_gate,
    w_up,
    w_down,
):
    anchor = jnp.dot(
        rms_scale(tokens[0].astype(jnp.float32), attn_gain).astype(jnp.bfloat16),
        q_weight,
        preferred_element_type=jnp.float32,
    )
    fetched, _ = fetch_slot(cache_kv, holder, anchor)
    down_all = lax.all_gather(w_down, "blk", axis=0, tiled=True)
    cache_keys = fetched[0]
    cache_vals = fetched[1]
    cache_length = cache_len[0]
    block_rows = tokens[0]
    first_pass = attend_block(
        block_rows,
        cache_keys,
        cache_vals,
        cache_length,
        attn_gain,
        q_weight,
        k_weight,
        v_weight,
        o_weight,
    )
    chosen_mask = accept[0] == 1
    block_len = block_rows.shape[0]
    kept = block_len // 2
    slot_of = jnp.cumsum(chosen_mask.astype(jnp.int32)) - 1
    hits = chosen_mask[None, :] & (slot_of[None, :] == jnp.arange(kept, dtype=jnp.int32)[:, None])
    kept_rows = jnp.sum(jnp.where(hits, jnp.arange(block_len, dtype=jnp.int32)[None, :], 0), axis=1)
    fnorm = rms_scale(first_pass, ffn_gain).astype(jnp.bfloat16)
    ffn_rows, down_all = lax.optimization_barrier((fnorm[kept_rows], down_all))
    ffn_kept = run_ffn(ffn_rows, w_gate, w_up, down_all, w_down.shape[0])
    ffn_sum = ffn_kept[jnp.clip(slot_of, 0, kept - 1)]
    placed = first_pass + ffn_sum
    second_in = jnp.where(chosen_mask[:, None], placed, block_rows.astype(jnp.float32))
    refined = attend_block(
        second_in,
        cache_keys,
        cache_vals,
        cache_length,
        attn_gain,
        q_weight,
        k_weight,
        v_weight,
        o_weight,
    )
    return refined[None]


def solution(mesh):
    return jax.shard_map(
        local,
        mesh=mesh,
        in_specs=(
            P(("req", "blk"), None, None),
            P(("req", "blk"), None, None, None),
            P(("req", "blk")),
            P(("req", "blk")),
            P(("req", "blk"), None),
            P(),
            P(),
            P(),
            P(),
            P(),
            P(),
            P(None, "blk"),
            P(None, "blk"),
            P("blk", None),
        ),
        out_specs=P(("req", "blk"), None, None),
        check_vma=False,
    )
```
